768 devices in a mesh: section: 48 (over z, x), ctx: 16 (over y, core).
Axes of the slice: x: 4, y: 8, z: 12, core: 2. Of those that a mesh axis runs over, the one named last changes fastest.
Arguments:
- residual_flow: float32 [48, 2048, 2048], P('section', 'ctx'), may hold values from -18 to 18
- tiers_each_segment: int32 [48], P('section'), may hold values from 0 to 1, as said below
- resident_tile_order: int32 [32], replicated, may hold values from 0 to 31, each once
- normalizer_weight_entries: float32 [48, 1, 2048], P('section'), may hold values from 0.1 to 1.9
- lookup_map_weights: bfloat16 [48, 1, 2048, 512], P('section'), may hold values from -2 to 2
- content_map_weights: bfloat16 [48, 1, 2048, 512], P('section'), may hold values from -0.125 to 0.125
- softmax_warmth: float32 [48, 1, 16], P('section'), may hold values from 2 to 320
- attention_result_weight: float32 [48, 1, 2048], P('section'), may hold values from 0.5 to 2
Outputs:
- passed: float32 [48, 2048, 2048], P('section', 'ctx')
The draws below stay inside these ranges and needn't reach their ends.
Inputs may be any that keep to these rules, and one draw needn't show every extreme that they name: `tiers_each_segment`: some section applies 1 layer and some none.
All inputs are finite; a program needn't handle non-finite values.
Results may differ from the reference program's by a relative error of at most 0.013.
Values may be sent and summed in bfloat16 or wider, within the bound.
No kernel may reach another device: no remote copies, remote signals or barrier semaphores. Data moves between devices by JAX's collectives and lax.ppermute only.
A program may use at most 64 MiB of HBM per device.

```python
import math
import jax
import jax.numpy as jnp
from jax import lax

H = 16
KEY_VALUE_HEADS = 4
ATTN_UNIT_WIDTH = 128
MAXL = 1
TOK_DEV = 128
D = 2048
KVD = 512
SEQ = 2048
HALF = 64
SECTIONS = 48
BLOCKS = 32


def draw_residual_flow(key, part):
    first_key = jax.random.fold_in(key, 0)
    return jnp.clip(jax.random.normal(first_key, (SECTIONS, SEQ, D), jnp.float32), -6.0, 6.0)


def draw_lookup_map_weights(key, part):
    noise = jnp.clip(jax.random.normal(key, (SECTIONS, MAXL, D, KVD), jnp.float32), -6.0, 6.0) * D ** (-0.5)
    return noise.astype(jnp.bfloat16)


def draw_softmax_warmth(key, part):
    upper = 24.0
    return jnp.exp(jax.random.uniform(key, (SECTIONS, MAXL, H), jnp.float32, math.log(2.0), math.log(upper)))


def draw_tiers_each_segment(key, part):
    first_key, second_key = jax.random.split(jax.random.fold_in(key, 7))
    counts = jax.random.randint(first_key, (SECTIONS,), 0, MAXL + 1)
    chosen = jax.random.randint(second_key, (), 0, SECTIONS)
    section_ids = jnp.arange(SECTIONS, dtype=jnp.int32)
    counts = jnp.where(section_ids == (chosen + 1) % SECTIONS, 0, counts)
    return jnp.where(section_ids == chosen, MAXL, counts).astype(jnp.int32)


def level_of(stream_key, extent, cuts, low, high):
    loudness = 1.0
    for dim, parts in cuts:
        draws = jax.random.uniform(jax.random.fold_in(jax.random.fold_in(stream_key, 6), dim), (parts,), jnp.float32, low / len(cuts), high / len(cuts))
        loudness = loudness * jnp.repeat(jnp.exp(draws), extent[dim] // parts).reshape((-1,) + (1,) * (len(extent) - 1 - dim))
    return loudness


def scatter_about(rng, dims, deviation, bound, cuts=(), kind=jnp.bfloat16):
    loudness = level_of(rng, dims, cuts, -0.22, 0.18) if cuts else 1.0
    result = jax.random.normal(rng, dims, jnp.float32) * deviation * loudness
    return jnp.minimum(jnp.maximum(result, -bound), bound).astype(kind)


def setup_inputs(seed: int = 0) -> dict:
    splits = jax.random.split(jax.random.key(seed), 9)
    residual_flow = draw_residual_flow(jax.random.fold_in(splits[8], 71), 0)
    tiers_each_segment = draw_tiers_each_segment(jax.random.fold_in(splits[8], 71), 0)
    resident_tile_order = jax.random.permutation(splits[2], BLOCKS).astype(jnp.int32)
    normalizer_weight_entries = jnp.clip(1.0 + 0.18 * jax.random.normal(splits[3], (SECTIONS, MAXL, D), jnp.float32), 0.1, 1.9)
    lookup_map_weights = draw_lookup_map_weights(jax.random.fold_in(splits[8], 71), 0)
    content_map_weights = scatter_about(splits[5], (SECTIONS, MAXL, D, KVD), D ** -0.5, 0.125, ((0, 48),))
    softmax_warmth = draw_softmax_warmth(jax.random.fold_in(splits[8], 71), 0)
    attention_result_weight = jnp.clip(jnp.exp(math.log(2.0) - 1.3862944 * jax.random.uniform(splits[7], (SECTIONS, MAXL, D), jnp.float32) ** level_of(splits[7], (SECTIONS, MAXL, D), ((0, 48),), -0.2, 0.2)), 0.5, 2.0)
    return dict(residual_flow=residual_flow, tiers_each_segment=tiers_each_segment, resident_tile_order=resident_tile_order, normalizer_weight_entries=normalizer_weight_entries, lookup_map_weights=lookup_map_weights, content_map_weights=content_map_weights, softmax_warmth=softmax_warmth, attention_result_weight=attention_result_weight)


def head_norm(values):
    return values * lax.rsqrt(lax.optimization_barrier(jnp.mean(values * values, axis=-1, keepdims=True)) + 1e-05)

def section_layer(stream_rows, positions, gain_row, key_mat, value_mat, temps, out_row):
    query_groups = H // KEY_VALUE_HEADS
    normed = (stream_rows * lax.rsqrt(lax.optimization_barrier(jnp.mean(stream_rows * stream_rows, axis=-1, keepdims=True)) + 1e-05) * gain_row).astype(jnp.bfloat16)
    keys_raw = jnp.dot(normed, key_mat, preferred_element_type=jnp.float32)
    key_unit = head_norm(keys_raw.reshape(SEQ, KEY_VALUE_HEADS, ATTN_UNIT_WIDTH)).astype(jnp.bfloat16)
    values = jnp.dot(normed, value_mat, preferred_element_type=jnp.float32).astype(jnp.bfloat16).reshape(SEQ, KEY_VALUE_HEADS, ATTN_UNIT_WIDTH)
    queries = head_norm(normed.astype(jnp.float32).reshape(SEQ, KEY_VALUE_HEADS, query_groups, ATTN_UNIT_WIDTH)).astype(jnp.bfloat16)
    scores = jnp.einsum('qcge,sce->qcgs', queries.astype(jnp.float32), key_unit.astype(jnp.float32), precision=lax.Precision.HIGHEST)
    scores = scores * (temps / ATTN_UNIT_WIDTH).reshape(1, KEY_VALUE_HEADS, query_groups, 1)
    allowed = (positions[None, :] <= positions[:, None])[:, None, None, :]
    scores = jnp.where(allowed, scores, -1e+30)
    row_max = lax.optimization_barrier(jnp.max(scores, axis=-1, keepdims=True))
    weights = jnp.where(allowed, jnp.exp(scores - row_max), 0.0)
    weight_sum = lax.optimization_barrier(jnp.sum(weights, axis=-1))
    mixed_out = jnp.einsum('qcgs,sce->qcge', weights.astype(jnp.bfloat16).astype(jnp.float32), values.astype(jnp.float32), precision=lax.Precision.HIGHEST)
    mixed_out = mixed_out / weight_sum[..., None]
    return stream_rows + out_row * mixed_out.reshape(SEQ, D)

def reference(residual_flow, tiers_each_segment, resident_tile_order, normalizer_weight_entries, lookup_map_weights, content_map_weights, softmax_warmth, attention_result_weight):
    row_ids = jnp.arange(SEQ, dtype=jnp.int32)
    slot_ids = row_ids // TOK_DEV * 2 + row_ids % TOK_DEV // HALF
    positions = resident_tile_order[slot_ids].astype(jnp.int32) * HALF + row_ids % HALF

    def advance_stack_segment(section_items):
        stream_rows, layer_count, gains, key_mats, value_mats, temps, out_rows = section_items
        for tier_ordinal in range(MAXL):
            updated = section_layer(stream_rows, positions, gains[tier_ordinal], key_mats[tier_ordinal], value_mats[tier_ordinal], temps[tier_ordinal], out_rows[tier_ordinal])
            stream_rows = jnp.where(tier_ordinal < layer_count, updated, stream_rows)
        return stream_rows
    segment_result = lax.map(advance_stack_segment, (residual_flow, tiers_each_segment, normalizer_weight_entries, lookup_map_weights, content_map_weights, softmax_warmth, attention_result_weight))
    return jnp.roll(segment_result, 1, axis=0)
```

```python
import jax
import jax.numpy as jnp
from jax import lax
from jax.sharding import PartitionSpec as P

H = 16
KEY_VALUE_HEADS = 4
ATTN_UNIT_WIDTH = 128


def passed_along(block, axis, distance):
    devices = range(lax.axis_size(axis))
    route = [((i - distance) % len(devices), i) for i in devices]
    return lax.ppermute(block, axis, route)


def head_norm(values):
    return values * lax.rsqrt(jnp.mean(values * values, axis=-1, keepdims=True) + 1e-05)


def row_positions(row_start, row_count, resident_tile_order, tok_rows):
    row_ids = row_start + jnp.arange(row_count, dtype=jnp.int32)
    half_rows = tok_rows // 2
    slot_ids = row_ids // tok_rows * 2 + row_ids % tok_rows // half_rows
    lookup = (
        slot_ids[:, None] == jnp.arange(resident_tile_order.shape[0], dtype=jnp.int32)[None, :]
    ).astype(jnp.int32)
    return jnp.sum(lookup * resident_tile_order[None, :], axis=1) * half_rows + row_ids % half_rows


def attend_block(running, block, key_pos, queries, logit_multiplier, query_pos):
    running_max, running_sum, running_acc = running
    rows = block.shape[0]
    kv_heads = queries.shape[0]
    kvd = block.shape[1] // 2
    key_piece = block[:, :kvd].reshape(rows, kv_heads, -1)
    value_piece = block[:, kvd:].reshape(rows, kv_heads, -1)
    allowed = (key_pos[None, :] <= query_pos[:, None])[None, None, :, :]
    scores = (
        jnp.einsum("cgqe,sce->cgqs", queries, key_piece, preferred_element_type=jnp.float32)
        * logit_multiplier
    )
    scores = jnp.where(allowed, scores, -1e30)
    new_max = jnp.maximum(running_max, jnp.max(scores, axis=-1))
    weights = jnp.where(allowed, jnp.exp(scores - new_max[..., None]), 0.0)
    scale = jnp.exp(running_max - new_max)
    new_sum = running_sum * scale + jnp.sum(weights, axis=-1)
    new_acc = running_acc * scale[..., None] + jnp.einsum(
        "cgqs,sce->cgqe",
        weights.astype(jnp.bfloat16),
        value_piece,
        preferred_element_type=jnp.float32,
    )
    return (new_max, new_sum, new_acc)


def local(
    residual_flow,
    tiers_each_segment,
    resident_tile_order,
    normalizer_weight_entries,
    lookup_map_weights,
    content_map_weights,
    softmax_warmth,
    attention_result_weight,
):
    tok_rows = residual_flow.shape[1]
    query_groups = H // KEY_VALUE_HEADS
    n_ctx = lax.axis_size("ctx")
    n_ring = n_ctx // 2
    me = lax.axis_index("ctx")
    chip = me // 2
    core = me % 2
    step_dir = 1 - 2 * core
    residual = residual_flow[0]
    query_pos = row_positions(me * tok_rows, tok_rows, resident_tile_order, tok_rows)
    normed = (
        residual
        * lax.rsqrt(jnp.mean(residual * residual, axis=-1, keepdims=True) + 1e-05)
        * normalizer_weight_entries[0, 0]
    ).astype(jnp.bfloat16)
    keys_raw = jnp.dot(normed, lookup_map_weights[0, 0], preferred_element_type=jnp.float32)
    key_unit = (
        head_norm(keys_raw.reshape(tok_rows, KEY_VALUE_HEADS, ATTN_UNIT_WIDTH))
        .astype(jnp.bfloat16)
        .reshape(tok_rows, KEY_VALUE_HEADS * ATTN_UNIT_WIDTH)
    )
    values = jnp.dot(normed, content_map_weights[0, 0], preferred_element_type=jnp.float32).astype(
        jnp.bfloat16
    )
    queries = head_norm(
        normed.astype(jnp.float32).reshape(tok_rows, KEY_VALUE_HEADS, query_groups, ATTN_UNIT_WIDTH)
    ).astype(jnp.bfloat16)
    queries = jnp.transpose(queries, (1, 2, 0, 3))
    logit_multiplier = (softmax_warmth[0, 0] / ATTN_UNIT_WIDTH).reshape(
        KEY_VALUE_HEADS, query_groups, 1, 1
    )
    own_block = jnp.concatenate([key_unit, values], axis=1)

    ring_route = [
        (i, ((i // 2 + (1 if i % 2 == 0 else -1)) % n_ring) * 2 + i % 2) for i in range(n_ctx)
    ]
    partner_route = [(i, i ^ 1) for i in range(n_ctx)]

    def origin_pos(origin):
        return row_positions(origin * tok_rows, tok_rows, resident_tile_order, tok_rows)

    def fold(running, block, origin):
        return attend_block(
            running, block, origin_pos(origin), queries, logit_multiplier, query_pos
        )

    running = (
        jnp.full((KEY_VALUE_HEADS, query_groups, tok_rows), -1e30, jnp.float32),
        jnp.zeros((KEY_VALUE_HEADS, query_groups, tok_rows), jnp.float32),
        jnp.zeros((KEY_VALUE_HEADS, query_groups, tok_rows, ATTN_UNIT_WIDTH), jnp.float32),
    )
    ring_block = own_block
    pending = None
    for step in range(n_ring):
        ring_origin = ((chip - step * step_dir) % n_ring) * 2 + core
        partner_origin = ((chip + step * step_dir) % n_ring) * 2 + (1 - core)
        partner_block = lax.ppermute(ring_block, "ctx", partner_route)
        next_block = None
        if step < n_ring - 1:
            next_block = lax.ppermute(ring_block, "ctx", ring_route)
        running = fold(running, ring_block, ring_origin)
        if pending is not None:
            running = fold(running, *pending)
        pending = (partner_block, partner_origin)
        ring_block = next_block
    running = fold(running, *pending)

    mixed_out = running[2] / running[1][..., None]
    mixed_rows = jnp.transpose(mixed_out, (2, 0, 1, 3)).reshape(
        tok_rows, KEY_VALUE_HEADS * query_groups * ATTN_UNIT_WIDTH
    )
    updated = residual + attention_result_weight[0, 0] * mixed_rows
    residual = jnp.where(0 < tiers_each_segment[0], updated, residual)
    return passed_along(residual[None], "section", 1)


def solution(mesh):
    in_specs = (
        P("section", "ctx", None),
        P("section"),
        P(),
        P("section", None, None),
        P("section", None, None, None),
        P("section", None, None, None),
        P("section", None, None),
        P("section", None, None),
    )
    out_specs = P("section", "ctx", None)
    return jax.shard_map(local, mesh=mesh, in_specs=in_specs, out_specs=out_specs, check_vma=False)
```

```python
import jax
import jax.numpy as jnp
from jax import lax
from jax.sharding import PartitionSpec as P

H = 16
KEY_VALUE_HEADS = 4
ATTN_UNIT_WIDTH = 128


def passed_along(block, axis, distance):
    devices = range(lax.axis_size(axis))
    route = [((i - distance) % len(devices), i) for i in devices]
    return lax.ppermute(block, axis, route)


def head_norm(values):
    return values * lax.rsqrt(jnp.mean(values * values, axis=-1, keepdims=True) + 1e-05)


def row_positions(row_start, row_count, resident_tile_order, tok_rows):
    row_ids = row_start + jnp.arange(row_count, dtype=jnp.int32)
    half_rows = tok_rows // 2
    slot_ids = row_ids // tok_rows * 2 + row_ids % tok_rows // half_rows
    lookup = (
        slot_ids[:, None] == jnp.arange(resident_tile_order.shape[0], dtype=jnp.int32)[None, :]
    ).astype(jnp.int32)
    return jnp.sum(lookup * resident_tile_order[None, :], axis=1) * half_rows + row_ids % half_rows


def attend_block(running, block, key_pos, queries, logit_multiplier, query_pos):
    running_max, running_sum, running_acc = running
    rows = block.shape[0]
    kv_heads = queries.shape[0]
    kvd = block.shape[1] // 2
    key_piece = block[:, :kvd].reshape(rows, kv_heads, -1)
    value_piece = block[:, kvd:].reshape(rows, kv_heads, -1)
    allowed = (key_pos[None, :] <= query_pos[:, None])[None, None, :, :]
    scores = (
        jnp.einsum("cgqe,sce->cgqs", queries, key_piece, preferred_element_type=jnp.float32)
        * logit_multiplier
    )
    scores = jnp.where(allowed, scores, -1e30)
    new_max = jnp.maximum(running_max, jnp.max(scores, axis=-1))
    weights = jnp.where(allowed, jnp.exp(scores - new_max[..., None]), 0.0)
    scale = jnp.exp(running_max - new_max)
    new_sum = running_sum * scale + jnp.sum(weights, axis=-1)
    new_acc = running_acc * scale[..., None] + jnp.einsum(
        "cgqs,sce->cgqe",
        weights.astype(jnp.bfloat16),
        value_piece,
        preferred_element_type=jnp.float32,
    )
    return (new_max, new_sum, new_acc)


def local(
    residual_flow,
    tiers_each_segment,
    resident_tile_order,
    normalizer_weight_entries,
    lookup_map_weights,
    content_map_weights,
    softmax_warmth,
    attention_result_weight,
):
    tok_rows = residual_flow.shape[1]
    query_groups = H // KEY_VALUE_HEADS
    n_ctx = lax.axis_size("ctx")
    n_ring = n_ctx // 2
    me = lax.axis_index("ctx")
    chip = me // 2
    core = me % 2
    step_dir = 1 - 2 * core
    residual = residual_flow[0]
    query_pos = row_positions(me * tok_rows, tok_rows, resident_tile_order, tok_rows)
    normed = (
        residual
        * lax.rsqrt(jnp.mean(residual * residual, axis=-1, keepdims=True) + 1e-05)
        * normalizer_weight_entries[0, 0]
    ).astype(jnp.bfloat16)
    keys_raw = jnp.dot(normed, lookup_map_weights[0, 0], preferred_element_type=jnp.float32)
    key_unit = (
        head_norm(keys_raw.reshape(tok_rows, KEY_VALUE_HEADS, ATTN_UNIT_WIDTH))
        .astype(jnp.bfloat16)
        .reshape(tok_rows, KEY_VALUE_HEADS * ATTN_UNIT_WIDTH)
    )
    values = jnp.dot(normed, content_map_weights[0, 0], preferred_element_type=jnp.float32).astype(
        jnp.bfloat16
    )
    queries = head_norm(
        normed.astype(jnp.float32).reshape(tok_rows, KEY_VALUE_HEADS, query_groups, ATTN_UNIT_WIDTH)
    ).astype(jnp.bfloat16)
    queries = jnp.transpose(queries, (1, 2, 0, 3))
    logit_multiplier = (softmax_warmth[0, 0] / ATTN_UNIT_WIDTH).reshape(
        KEY_VALUE_HEADS, query_groups, 1, 1
    )
    own_block = jnp.concatenate([key_unit, values], axis=1)

    same_core = [list(range(c, n_ctx, 2)) for c in range(2)]
    partner_route = [(i, i ^ 1) for i in range(n_ctx)]
    mine = lax.all_gather(own_block, "ctx", axis=0, tiled=True, axis_index_groups=same_core)
    theirs = lax.ppermute(mine, "ctx", partner_route)

    def group_pos(group_core):
        origins = jnp.arange(n_ring, dtype=jnp.int32) * 2 + group_core
        return jnp.concatenate(
            [row_positions(origins[j] * tok_rows, tok_rows, resident_tile_order, tok_rows) for j in range(n_ring)]
        )

    running = (
        jnp.full((KEY_VALUE_HEADS, query_groups, tok_rows), -1e30, jnp.float32),
        jnp.zeros((KEY_VALUE_HEADS, query_groups, tok_rows), jnp.float32),
        jnp.zeros((KEY_VALUE_HEADS, query_groups, tok_rows, ATTN_UNIT_WIDTH), jnp.float32),
    )
    running = attend_block(running, mine, group_pos(core), queries, logit_multiplier, query_pos)
    running = attend_block(running, theirs, group_pos(1 - core), queries, logit_multiplier, query_pos)

    mixed_out = running[2] / running[1][..., None]
    mixed_rows = jnp.transpose(mixed_out, (2, 0, 1, 3)).reshape(
        tok_rows, KEY_VALUE_HEADS * query_groups * ATTN_UNIT_WIDTH
    )
    updated = residual + attention_result_weight[0, 0] * mixed_rows
    residual = jnp.where(0 < tiers_each_segment[0], updated, residual)
    return passed_along(residual[None], "section", 1)


def solution(mesh):
    in_specs = (
        P("section", "ctx", None),
        P("section"),
        P(),
        P("section", None, None),
        P("section", None, None, None),
        P("section", None, None, None),
        P("section", None, None),
        P("section", None, None),
    )
    out_specs = P("section", "ctx", None)
    return jax.shard_map(local, mesh=mesh, in_specs=in_specs, out_specs=out_specs, check_vma=False)
```

```python
import functools

import jax
import jax.numpy as jnp
from jax import lax
from jax.experimental import pallas as pl
from jax.experimental.pallas import tpu as pltpu
from jax.sharding import PartitionSpec as P

H = 16
KEY_VALUE_HEADS = 4
ATTN_UNIT_WIDTH = 128


def passed_along(block, axis, distance):
    devices = range(lax.axis_size(axis))
    route = [((i - distance) % len(devices), i) for i in devices]
    return lax.ppermute(block, axis, route)


def head_norm(values):
    return values * lax.rsqrt(jnp.mean(values * values, axis=-1, keepdims=True) + 1e-05)


def attention_kernel(
    mult_ref, tiers_ref, qpos_ref, kpos_a_ref, kpos_b_ref, q_ref,
    ka_ref, va_ref, kb_ref, vb_ref, x_ref, w_ref, out_ref,
):
    c = pl.program_id(0)
    group = q_ref.shape[1] // ATTN_UNIT_WIDTH
    qpos = qpos_ref[...]
    allowed_a = kpos_a_ref[...] <= qpos
    allowed_b = kpos_b_ref[...] <= qpos
    ka = ka_ref[...]
    kb = kb_ref[...]
    va = va_ref[...]
    vb = vb_ref[...]
    gate = tiers_ref[0] > 0
    dims = (((1,), (1,)), ((), ()))
    for g in range(group):
        cols = slice(g * ATTN_UNIT_WIDTH, (g + 1) * ATTN_UNIT_WIDTH)
        qh = q_ref[:, cols]
        mult = mult_ref[c * group + g]
        s_a = lax.dot_general(qh, ka, dims, preferred_element_type=jnp.float32) * mult
        s_b = lax.dot_general(qh, kb, dims, preferred_element_type=jnp.float32) * mult
        s_a = jnp.where(allowed_a, s_a, -1e30)
        s_b = jnp.where(allowed_b, s_b, -1e30)
        row_max = jnp.maximum(
            jnp.max(s_a, axis=1, keepdims=True), jnp.max(s_b, axis=1, keepdims=True)
        )
        p_a = jnp.where(allowed_a, jnp.exp(s_a - row_max), 0.0)
        p_b = jnp.where(allowed_b, jnp.exp(s_b - row_max), 0.0)
        total = jnp.sum(p_a, axis=1, keepdims=True) + jnp.sum(p_b, axis=1, keepdims=True)
        mixed = jnp.dot(
            p_a.astype(jnp.bfloat16), va, preferred_element_type=jnp.float32
        ) + jnp.dot(p_b.astype(jnp.bfloat16), vb, preferred_element_type=jnp.float32)
        mixed = mixed / total
        x = x_ref[:, cols]
        out_ref[:, cols] = jnp.where(gate, x + w_ref[:, cols] * mixed, x)


def attend_and_update(mult, tiers, qpos, kpos_a, kpos_b, queries, block_a, block_b, x, w_out):
    rows, width = x.shape
    kv_rows = block_a.shape[0]
    kv_heads = KEY_VALUE_HEADS
    head_cols = width // kv_heads
    smem = pl.BlockSpec(memory_space=pltpu.SMEM)
    whole = lambda shape: pl.BlockSpec(shape, lambda c: (0, 0))
    cols = lambda shape: pl.BlockSpec(shape, lambda c: (0, c))
    values_at = lambda shape: pl.BlockSpec(shape, lambda c: (0, c + kv_heads))
    kv_block = (kv_rows, ATTN_UNIT_WIDTH)
    flops = 4 * rows * 2 * kv_rows * ATTN_UNIT_WIDTH * H
    return pl.pallas_call(
        attention_kernel,
        grid=(kv_heads,),
        in_specs=[
            smem,
            smem,
            whole((rows, 1)),
            whole((1, kv_rows)),
            whole((1, kv_rows)),
            cols((rows, head_cols)),
            cols(kv_block),
            values_at(kv_block),
            cols(kv_block),
            values_at(kv_block),
            cols((rows, head_cols)),
            cols((1, head_cols)),
        ],
        out_specs=cols((rows, head_cols)),
        out_shape=jax.ShapeDtypeStruct((rows, width), jnp.float32),
        cost_estimate=pl.CostEstimate(
            flops=flops,
            transcendentals=rows * 2 * kv_rows * H,
            bytes_accessed=4 * kv_rows * 1024 + rows * width * 10,
        ),
    )(mult, tiers, qpos, kpos_a, kpos_b, queries, block_a, block_a, block_b, block_b, x, w_out)


def local(
    residual_flow,
    tiers_each_segment,
    resident_tile_order,
    normalizer_weight_entries,
    lookup_map_weights,
    content_map_weights,
    softmax_warmth,
    attention_result_weight,
):
    tok_rows = residual_flow.shape[1]
    query_groups = H // KEY_VALUE_HEADS
    n_ctx = lax.axis_size("ctx")
    n_chips = n_ctx // 2
    me = lax.axis_index("ctx")
    core = me % 2
    half_rows = tok_rows // 2
    residual = residual_flow[0]

    all_pos = (
        jnp.repeat(resident_tile_order.astype(jnp.int32), half_rows) * half_rows
        + jnp.tile(jnp.arange(half_rows, dtype=jnp.int32), resident_tile_order.shape[0])
    )
    query_pos = lax.dynamic_slice(all_pos, (me * tok_rows,), (tok_rows,)).reshape(tok_rows, 1)
    by_core = all_pos.reshape(n_chips, 2, tok_rows)
    pos_mine = lax.dynamic_index_in_dim(by_core, core, axis=1, keepdims=False).reshape(1, -1)
    pos_theirs = lax.dynamic_index_in_dim(by_core, 1 - core, axis=1, keepdims=False).reshape(1, -1)

    normed = (
        residual
        * lax.rsqrt(jnp.mean(residual * residual, axis=-1, keepdims=True) + 1e-05)
        * normalizer_weight_entries[0, 0]
    ).astype(jnp.bfloat16)
    keys_raw = jnp.dot(normed, lookup_map_weights[0, 0], preferred_element_type=jnp.float32)
    key_unit = (
        head_norm(keys_raw.reshape(tok_rows, KEY_VALUE_HEADS, ATTN_UNIT_WIDTH))
        .astype(jnp.bfloat16)
        .reshape(tok_rows, KEY_VALUE_HEADS * ATTN_UNIT_WIDTH)
    )
    values = jnp.dot(normed, content_map_weights[0, 0], preferred_element_type=jnp.float32).astype(
        jnp.bfloat16
    )
    queries = (
        head_norm(normed.astype(jnp.float32).reshape(tok_rows, H, ATTN_UNIT_WIDTH))
        .astype(jnp.bfloat16)
        .reshape(tok_rows, H * ATTN_UNIT_WIDTH)
    )
    own_block = jnp.concatenate([key_unit, values], axis=1)

    same_core = [list(range(c, n_ctx, 2)) for c in range(2)]
    partner_route = [(i, i ^ 1) for i in range(n_ctx)]
    mine = lax.all_gather(own_block, "ctx", axis=0, tiled=True, axis_index_groups=same_core)
    theirs = lax.ppermute(mine, "ctx", partner_route)

    mult = softmax_warmth[0, 0] / ATTN_UNIT_WIDTH
    residual = attend_and_update(
        mult,
        tiers_each_segment,
        query_pos,
        pos_mine,
        pos_theirs,
        queries,
        mine,
        theirs,
        residual,
        attention_result_weight[0],
    )
    return passed_along(residual[None], "section", 1)


def solution(mesh):
    in_specs = (
        P("section", "ctx", None),
        P("section"),
        P(),
        P("section", None, None),
        P("section", None, None, None),
        P("section", None, None, None),
        P("section", None, None),
        P("section", None, None),
    )
    out_specs = P("section", "ctx", None)
    return jax.shard_map(local, mesh=mesh, in_specs=in_specs, out_specs=out_specs, check_vma=False)
```

```python
import functools

import jax
import jax.numpy as jnp
from jax import lax
from jax.experimental import pallas as pl
from jax.experimental.pallas import tpu as pltpu
from jax.sharding import PartitionSpec as P

H = 16
KEY_VALUE_HEADS = 4
ATTN_UNIT_WIDTH = 128


def passed_along(block, axis, distance):
    devices = range(lax.axis_size(axis))
    route = [((i - distance) % len(devices), i) for i in devices]
    return lax.ppermute(block, axis, route)


def head_norm(values):
    return values * lax.rsqrt(jnp.mean(values * values, axis=-1, keepdims=True) + 1e-05)


def attention_kernel(
    mult_ref, tiers_ref, qpos_ref, kpos_a_ref, kpos_b_ref, q_ref,
    ka_ref, va_ref, kb_ref, vb_ref, x_ref, w_ref, out_ref,
):
    c = pl.program_id(0)
    group = q_ref.shape[1] // ATTN_UNIT_WIDTH
    qpos = qpos_ref[...]
    allowed_a = kpos_a_ref[...] <= qpos
    allowed_b = kpos_b_ref[...] <= qpos
    ka = ka_ref[...]
    kb = kb_ref[...]
    va = va_ref[...]
    vb = vb_ref[...]
    gate = tiers_ref[0] > 0
    dims = (((1,), (1,)), ((), ()))
    for g in range(group):
        cols = slice(g * ATTN_UNIT_WIDTH, (g + 1) * ATTN_UNIT_WIDTH)
        qh = q_ref[:, cols]
        mult = mult_ref[c * group + g]
        s_a = jnp.where(allowed_a, lax.dot_general(qh, ka, dims, preferred_element_type=jnp.float32), -1e30)
        s_b = jnp.where(allowed_b, lax.dot_general(qh, kb, dims, preferred_element_type=jnp.float32), -1e30)
        row_max = jnp.maximum(
            jnp.max(s_a, axis=1, keepdims=True), jnp.max(s_b, axis=1, keepdims=True)
        ) * mult
        p_a = jnp.exp(s_a * mult - row_max)
        p_b = jnp.exp(s_b * mult - row_max)
        total = jnp.sum(p_a, axis=1, keepdims=True) + jnp.sum(p_b, axis=1, keepdims=True)
        mixed = jnp.dot(
            p_a.astype(jnp.bfloat16), va, preferred_element_type=jnp.float32
        ) + jnp.dot(p_b.astype(jnp.bfloat16), vb, preferred_element_type=jnp.float32)
        mixed = mixed / total
        x = x_ref[:, cols]
        out_ref[:, cols] = jnp.where(gate, x + w_ref[:, cols] * mixed, x)


def prologue_kernel(x_ref, gain_ref, wk_ref, wv_ref, kv_ref, q_ref):
    x = x_ref[...]
    normed = (
        x * lax.rsqrt(jnp.mean(x * x, axis=1, keepdims=True) + 1e-05) * gain_ref[...]
    ).astype(jnp.bfloat16)
    keys = jnp.dot(normed, wk_ref[...], preferred_element_type=jnp.float32)
    kv_cols = keys.shape[1]
    for c in range(kv_cols // ATTN_UNIT_WIDTH):
        cols = slice(c * ATTN_UNIT_WIDTH, (c + 1) * ATTN_UNIT_WIDTH)
        kv_ref[:, cols] = head_norm(keys[:, cols]).astype(jnp.bfloat16)
    kv_ref[:, kv_cols:] = jnp.dot(
        normed, wv_ref[...], preferred_element_type=jnp.float32
    ).astype(jnp.bfloat16)
    wide = normed.astype(jnp.float32)
    for h in range(wide.shape[1] // ATTN_UNIT_WIDTH):
        cols = slice(h * ATTN_UNIT_WIDTH, (h + 1) * ATTN_UNIT_WIDTH)
        q_ref[:, cols] = head_norm(wide[:, cols]).astype(jnp.bfloat16)


def prologue(x, gain, wk, wv):
    rows, width = x.shape
    kv_cols = wk.shape[1]
    return pl.pallas_call(
        prologue_kernel,
        out_shape=(
            jax.ShapeDtypeStruct((rows, 2 * kv_cols), jnp.bfloat16),
            jax.ShapeDtypeStruct((rows, width), jnp.bfloat16),
        ),
        cost_estimate=pl.CostEstimate(
            flops=4 * rows * width * kv_cols,
            transcendentals=rows * 24,
            bytes_accessed=2 * width * kv_cols * 2 + rows * width * 6 + rows * kv_cols * 4,
        ),
    )(x, gain, wk, wv)


def attend_and_update(mult, tiers, qpos, kpos_a, kpos_b, queries, block_a, block_b, x, w_out):
    rows, width = x.shape
    kv_rows = block_a.shape[0]
    kv_heads = KEY_VALUE_HEADS
    head_cols = width // kv_heads
    smem = pl.BlockSpec(memory_space=pltpu.SMEM)
    whole = lambda shape: pl.BlockSpec(shape, lambda c: (0, 0))
    cols = lambda shape: pl.BlockSpec(shape, lambda c: (0, c))
    values_at = lambda shape: pl.BlockSpec(shape, lambda c: (0, c + kv_heads))
    kv_block = (kv_rows, ATTN_UNIT_WIDTH)
    flops = 4 * rows * 2 * kv_rows * ATTN_UNIT_WIDTH * H
    return pl.pallas_call(
        attention_kernel,
        grid=(kv_heads,),
        in_specs=[
            smem,
            smem,
            whole((rows, 1)),
            whole((1, kv_rows)),
            whole((1, kv_rows)),
            cols((rows, head_cols)),
            cols(kv_block),
            values_at(kv_block),
            cols(kv_block),
            values_at(kv_block),
            cols((rows, head_cols)),
            cols((1, head_cols)),
        ],
        out_specs=cols((rows, head_cols)),
        out_shape=jax.ShapeDtypeStruct((rows, width), jnp.float32),
        cost_estimate=pl.CostEstimate(
            flops=flops,
            transcendentals=rows * 2 * kv_rows * H,
            bytes_accessed=4 * kv_rows * 1024 + rows * width * 10,
        ),
    )(mult, tiers, qpos, kpos_a, kpos_b, queries, block_a, block_a, block_b, block_b, x, w_out)


def local(
    residual_flow,
    tiers_each_segment,
    resident_tile_order,
    normalizer_weight_entries,
    lookup_map_weights,
    content_map_weights,
    softmax_warmth,
    attention_result_weight,
):
    tok_rows = residual_flow.shape[1]
    n_ctx = lax.axis_size("ctx")
    n_chips = n_ctx // 2
    me = lax.axis_index("ctx")
    core = me % 2
    half_rows = tok_rows // 2
    residual = residual_flow[0]

    all_pos = (
        jnp.repeat(resident_tile_order.astype(jnp.int32), half_rows) * half_rows
        + jnp.tile(jnp.arange(half_rows, dtype=jnp.int32), resident_tile_order.shape[0])
    )
    query_pos = lax.dynamic_slice(all_pos, (me * tok_rows,), (tok_rows,)).reshape(tok_rows, 1)
    by_core = all_pos.reshape(n_chips, 2, tok_rows)
    pos_mine = lax.dynamic_index_in_dim(by_core, core, axis=1, keepdims=False).reshape(1, -1)
    pos_theirs = lax.dynamic_index_in_dim(by_core, 1 - core, axis=1, keepdims=False).reshape(1, -1)

    own_block, queries = prologue(
        residual,
        normalizer_weight_entries[0],
        lookup_map_weights[0, 0],
        content_map_weights[0, 0],
    )
    mult = softmax_warmth[0, 0] / ATTN_UNIT_WIDTH
    own_block, queries, query_pos, pos_mine, pos_theirs, mult = lax.optimization_barrier(
        (own_block, queries, query_pos, pos_mine, pos_theirs, mult)
    )

    same_core = [list(range(c, n_ctx, 2)) for c in range(2)]
    partner_route = [(i, i ^ 1) for i in range(n_ctx)]
    mine = lax.all_gather(own_block, "ctx", axis=0, tiled=True, axis_index_groups=same_core)
    theirs = lax.ppermute(mine, "ctx", partner_route)

    residual = attend_and_update(
        mult,
        tiers_each_segment,
        query_pos,
        pos_mine,
        pos_theirs,
        queries,
        mine,
        theirs,
        residual,
        attention_result_weight[0],
    )
    return passed_along(residual[None], "section", 1)


def solution(mesh):
    in_specs = (
        P("section", "ctx", None),
        P("section"),
        P(),
        P("section", None, None),
        P("section", None, None, None),
        P("section", None, None, None),
        P("section", None, None),
        P("section", None, None),
    )
    out_specs = P("section", "ctx", None)
    return jax.shard_map(local, mesh=mesh, in_specs=in_specs, out_specs=out_specs, check_vma=False)
```

```python
import functools

import jax
import jax.numpy as jnp
from jax import lax
from jax.experimental import pallas as pl
from jax.experimental.pallas import tpu as pltpu
from jax.sharding import PartitionSpec as P

H = 16
KEY_VALUE_HEADS = 4
ATTN_UNIT_WIDTH = 128


def passed_along(block, axis, distance):
    devices = range(lax.axis_size(axis))
    route = [((i - distance) % len(devices), i) for i in devices]
    return lax.ppermute(block, axis, route)


def head_norm(values):
    return values * lax.rsqrt(jnp.mean(values * values, axis=-1, keepdims=True) + 1e-05)


def first_half_kernel(mult_ref, qpos_ref, kpos_ref, q_ref, k_ref, v_ref, m_ref, l_ref, acc_ref):
    c = pl.program_id(0)
    group = q_ref.shape[1] // ATTN_UNIT_WIDTH
    allowed = kpos_ref[...] <= qpos_ref[...]
    k = k_ref[...]
    v = v_ref[...]
    dims = (((1,), (1,)), ((), ()))
    for g in range(group):
        cols = slice(g * ATTN_UNIT_WIDTH, (g + 1) * ATTN_UNIT_WIDTH)
        mult = mult_ref[c * group + g]
        s = jnp.where(allowed, lax.dot_general(q_ref[:, cols], k, dims, preferred_element_type=jnp.float32), -1e30)
        row_max = jnp.max(s, axis=1, keepdims=True) * mult
        p = jnp.exp(s * mult - row_max)
        m_ref[:, cols] = jnp.broadcast_to(row_max, (row_max.shape[0], ATTN_UNIT_WIDTH))
        l_ref[:, cols] = jnp.broadcast_to(jnp.sum(p, axis=1, keepdims=True), (p.shape[0], ATTN_UNIT_WIDTH))
        acc_ref[:, cols] = jnp.dot(p.astype(jnp.bfloat16), v, preferred_element_type=jnp.float32)


def second_half_kernel(
    mult_ref, tiers_ref, qpos_ref, kpos_ref, q_ref, k_ref, v_ref, m_ref, l_ref, acc_ref,
    x_ref, w_ref, out_ref,
):
    c = pl.program_id(0)
    group = q_ref.shape[1] // ATTN_UNIT_WIDTH
    allowed = kpos_ref[...] <= qpos_ref[...]
    k = k_ref[...]
    v = v_ref[...]
    gate = tiers_ref[0] > 0
    dims = (((1,), (1,)), ((), ()))
    for g in range(group):
        cols = slice(g * ATTN_UNIT_WIDTH, (g + 1) * ATTN_UNIT_WIDTH)
        mult = mult_ref[c * group + g]
        s = jnp.where(allowed, lax.dot_general(q_ref[:, cols], k, dims, preferred_element_type=jnp.float32), -1e30)
        old_max = m_ref[:, cols][:, :1]
        row_max = jnp.maximum(old_max, jnp.max(s, axis=1, keepdims=True) * mult)
        p = jnp.exp(s * mult - row_max)
        scale = jnp.exp(old_max - row_max)
        total = l_ref[:, cols] * scale + jnp.sum(p, axis=1, keepdims=True)
        mixed = acc_ref[:, cols] * scale + jnp.dot(
            p.astype(jnp.bfloat16), v, preferred_element_type=jnp.float32
        )
        mixed = mixed / total
        x = x_ref[:, cols]
        out_ref[:, cols] = jnp.where(gate, x + w_ref[:, cols] * mixed, x)


def prologue_kernel(x_ref, gain_ref, wk_ref, wv_ref, kv_ref, q_ref):
    x = x_ref[...]
    normed = (
        x * lax.rsqrt(jnp.mean(x * x, axis=1, keepdims=True) + 1e-05) * gain_ref[...]
    ).astype(jnp.bfloat16)
    keys = jnp.dot(normed, wk_ref[...], preferred_element_type=jnp.float32)
    kv_cols = keys.shape[1]
    for c in range(kv_cols // ATTN_UNIT_WIDTH):
        cols = slice(c * ATTN_UNIT_WIDTH, (c + 1) * ATTN_UNIT_WIDTH)
        kv_ref[:, cols] = head_norm(keys[:, cols]).astype(jnp.bfloat16)
    kv_ref[:, kv_cols:] = jnp.dot(
        normed, wv_ref[...], preferred_element_type=jnp.float32
    ).astype(jnp.bfloat16)
    wide = normed.astype(jnp.float32)
    for h in range(wide.shape[1] // ATTN_UNIT_WIDTH):
        cols = slice(h * ATTN_UNIT_WIDTH, (h + 1) * ATTN_UNIT_WIDTH)
        q_ref[:, cols] = head_norm(wide[:, cols]).astype(jnp.bfloat16)


def prologue(x, gain, wk, wv):
    rows, width = x.shape
    kv_cols = wk.shape[1]
    return pl.pallas_call(
        prologue_kernel,
        out_shape=(
            jax.ShapeDtypeStruct((rows, 2 * kv_cols), jnp.bfloat16),
            jax.ShapeDtypeStruct((rows, width), jnp.bfloat16),
        ),
        cost_estimate=pl.CostEstimate(
            flops=4 * rows * width * kv_cols,
            transcendentals=rows * 24,
            bytes_accessed=2 * width * kv_cols * 2 + rows * width * 6 + rows * kv_cols * 4,
        ),
    )(x, gain, wk, wv)


def attend_and_update(mult, tiers, qpos, kpos_a, kpos_b, queries, block_a, block_b, x, w_out):
    rows, width = x.shape
    kv_rows = block_a.shape[0]
    kv_heads = KEY_VALUE_HEADS
    head_cols = width // kv_heads
    smem = pl.BlockSpec(memory_space=pltpu.SMEM)
    whole = lambda shape: pl.BlockSpec(shape, lambda c: (0, 0))
    cols = lambda shape: pl.BlockSpec(shape, lambda c: (0, c))
    values_at = lambda shape: pl.BlockSpec(shape, lambda c: (0, c + kv_heads))
    kv_block = (kv_rows, ATTN_UNIT_WIDTH)
    wide = cols((rows, head_cols))
    state = jax.ShapeDtypeStruct((rows, width), jnp.float32)
    flops = 4 * rows * kv_rows * ATTN_UNIT_WIDTH * H
    cost = pl.CostEstimate(
        flops=flops, transcendentals=rows * kv_rows * H, bytes_accessed=2 * kv_rows * 1024 + rows * width * 16
    )
    running = pl.pallas_call(
        first_half_kernel,
        grid=(kv_heads,),
        in_specs=[smem, whole((rows, 1)), whole((1, kv_rows)), wide, cols(kv_block), values_at(kv_block)],
        out_specs=[wide, wide, wide],
        out_shape=[state, state, state],
        cost_estimate=cost,
    )(mult, qpos, kpos_a, queries, block_a, block_a)
    return pl.pallas_call(
        second_half_kernel,
        grid=(kv_heads,),
        in_specs=[
            smem, smem, whole((rows, 1)), whole((1, kv_rows)), wide, cols(kv_block), values_at(kv_block),
            wide, wide, wide, wide, cols((1, head_cols)),
        ],
        out_specs=wide,
        out_shape=state,
        cost_estimate=cost,
    )(mult, tiers, qpos, kpos_b, queries, block_b, block_b, *running, x, w_out)


def local(
    residual_flow,
    tiers_each_segment,
    resident_tile_order,
    normalizer_weight_entries,
    lookup_map_weights,
    content_map_weights,
    softmax_warmth,
    attention_result_weight,
):
    tok_rows = residual_flow.shape[1]
    n_ctx = lax.axis_size("ctx")
    n_chips = n_ctx // 2
    me = lax.axis_index("ctx")
    core = me % 2
    half_rows = tok_rows // 2
    residual = residual_flow[0]

    all_pos = (
        jnp.repeat(resident_tile_order.astype(jnp.int32), half_rows) * half_rows
        + jnp.tile(jnp.arange(half_rows, dtype=jnp.int32), resident_tile_order.shape[0])
    )
    query_pos = lax.dynamic_slice(all_pos, (me * tok_rows,), (tok_rows,)).reshape(tok_rows, 1)
    by_core = all_pos.reshape(n_chips, 2, tok_rows)
    pos_mine = lax.dynamic_index_in_dim(by_core, core, axis=1, keepdims=False).reshape(1, -1)
    pos_theirs = lax.dynamic_index_in_dim(by_core, 1 - core, axis=1, keepdims=False).reshape(1, -1)

    own_block, queries = prologue(
        residual,
        normalizer_weight_entries[0],
        lookup_map_weights[0, 0],
        content_map_weights[0, 0],
    )
    mult = softmax_warmth[0, 0] / ATTN_UNIT_WIDTH
    own_block, queries, query_pos, pos_mine, pos_theirs, mult = lax.optimization_barrier(
        (own_block, queries, query_pos, pos_mine, pos_theirs, mult)
    )

    same_core = [list(range(c, n_ctx, 2)) for c in range(2)]
    partner_route = [(i, i ^ 1) for i in range(n_ctx)]
    mine = lax.all_gather(own_block, "ctx", axis=0, tiled=True, axis_index_groups=same_core)
    theirs = lax.ppermute(mine, "ctx", partner_route)

    residual = attend_and_update(
        mult,
        tiers_each_segment,
        query_pos,
        pos_mine,
        pos_theirs,
        queries,
        mine,
        theirs,
        residual,
        attention_result_weight[0],
    )
    return passed_along(residual[None], "section", 1)


def solution(mesh):
    in_specs = (
        P("section", "ctx", None),
        P("section"),
        P(),
        P("section", None, None),
        P("section", None, None, None),
        P("section", None, None, None),
        P("section", None, None),
        P("section", None, None),
    )
    out_specs = P("section", "ctx", None)
    return jax.shard_map(local, mesh=mesh, in_specs=in_specs, out_specs=out_specs, check_vma=False)
```

```python
import functools

import jax
import jax.numpy as jnp
from jax import lax
from jax.experimental import pallas as pl
from jax.experimental.pallas import tpu as pltpu
from jax.sharding import PartitionSpec as P

H = 16
KEY_VALUE_HEADS = 4
ATTN_UNIT_WIDTH = 128


def passed_along(block, axis, distance):
    devices = range(lax.axis_size(axis))
    route = [((i - distance) % len(devices), i) for i in devices]
    return lax.ppermute(block, axis, route)


def head_norm(values):
    return values * lax.rsqrt(jnp.mean(values * values, axis=-1, keepdims=True) + 1e-05)


def attention_kernel(
    mult_ref, tiers_ref, qpos_ref, kpos_a_ref, kpos_b_ref, q_ref,
    ka_ref, va_ref, kb_ref, vb_ref, x_ref, w_ref, out_ref,
):
    c = pl.program_id(0)
    group = q_ref.shape[1] // ATTN_UNIT_WIDTH
    qpos = qpos_ref[...]
    allowed_a = kpos_a_ref[...] <= qpos
    allowed_b = kpos_b_ref[...] <= qpos
    ka = ka_ref[...]
    kb = kb_ref[...]
    va = va_ref[...]
    vb = vb_ref[...]
    gate = tiers_ref[0] > 0
    dims = (((1,), (1,)), ((), ()))
    for g in range(group):
        cols = slice(g * ATTN_UNIT_WIDTH, (g + 1) * ATTN_UNIT_WIDTH)
        qh = q_ref[:, cols]
        mult = mult_ref[c * group + g]
        s_a = jnp.where(allowed_a, lax.dot_general(qh, ka, dims, preferred_element_type=jnp.float32), -1e30)
        s_b = jnp.where(allowed_b, lax.dot_general(qh, kb, dims, preferred_element_type=jnp.float32), -1e30)
        row_max = jnp.maximum(
            jnp.max(s_a, axis=1, keepdims=True), jnp.max(s_b, axis=1, keepdims=True)
        ) * mult
        p_a = jnp.exp(s_a * mult - row_max)
        p_b = jnp.exp(s_b * mult - row_max)
        total = jnp.sum(p_a, axis=1, keepdims=True) + jnp.sum(p_b, axis=1, keepdims=True)
        mixed = jnp.dot(
            p_a.astype(jnp.bfloat16), va, preferred_element_type=jnp.float32
        ) + jnp.dot(p_b.astype(jnp.bfloat16), vb, preferred_element_type=jnp.float32)
        mixed = mixed / total
        x = x_ref[:, cols]
        out_ref[:, cols] = jnp.where(gate, x + w_ref[:, cols] * mixed, x)


def prologue_kernel(x_ref, gain_ref, wk_ref, wv_ref, kv_ref, q_ref):
    x = x_ref[...]
    normed = (
        x * lax.rsqrt(jnp.mean(x * x, axis=1, keepdims=True) + 1e-05) * gain_ref[...]
    ).astype(jnp.bfloat16)
    keys = jnp.dot(normed, wk_ref[...], preferred_element_type=jnp.float32)
    kv_cols = keys.shape[1]
    for c in range(kv_cols // ATTN_UNIT_WIDTH):
        cols = slice(c * ATTN_UNIT_WIDTH, (c + 1) * ATTN_UNIT_WIDTH)
        kv_ref[:, cols] = head_norm(keys[:, cols]).astype(jnp.bfloat16)
    kv_ref[:, kv_cols:] = jnp.dot(
        normed, wv_ref[...], preferred_element_type=jnp.float32
    ).astype(jnp.bfloat16)
    wide = normed.astype(jnp.float32)
    for h in range(wide.shape[1] // ATTN_UNIT_WIDTH):
        cols = slice(h * ATTN_UNIT_WIDTH, (h + 1) * ATTN_UNIT_WIDTH)
        q_ref[:, cols] = head_norm(wide[:, cols]).astype(jnp.bfloat16)


def prologue(x, gain, wk, wv):
    rows, width = x.shape
    kv_cols = wk.shape[1]
    return pl.pallas_call(
        prologue_kernel,
        out_shape=(
            jax.ShapeDtypeStruct((rows, 2 * kv_cols), jnp.bfloat16),
            jax.ShapeDtypeStruct((rows, width), jnp.bfloat16),
        ),
        cost_estimate=pl.CostEstimate(
            flops=4 * rows * width * kv_cols,
            transcendentals=rows * 24,
            bytes_accessed=2 * width * kv_cols * 2 + rows * width * 6 + rows * kv_cols * 4,
        ),
    )(x, gain, wk, wv)


def attend_and_update(mult, tiers, qpos, kpos_a, kpos_b, queries, block_a, block_b, x, w_out):
    rows, width = x.shape
    kv_rows = block_a.shape[0]
    kv_heads = KEY_VALUE_HEADS
    head_cols = width // kv_heads
    smem = pl.BlockSpec(memory_space=pltpu.SMEM)
    whole = lambda shape: pl.BlockSpec(shape, lambda c: (0, 0))
    cols = lambda shape: pl.BlockSpec(shape, lambda c: (0, c))
    values_at = lambda shape: pl.BlockSpec(shape, lambda c: (0, c + kv_heads))
    kv_block = (kv_rows, ATTN_UNIT_WIDTH)
    flops = 4 * rows * 2 * kv_rows * ATTN_UNIT_WIDTH * H
    return pl.pallas_call(
        attention_kernel,
        grid=(kv_heads,),
        in_specs=[
            smem,
            smem,
            whole((rows, 1)),
            whole((1, kv_rows)),
            whole((1, kv_rows)),
            cols((rows, head_cols)),
            cols(kv_block),
            values_at(kv_block),
            cols(kv_block),
            values_at(kv_block),
            cols((rows, head_cols)),
            cols((1, head_cols)),
        ],
        out_specs=cols((rows, head_cols)),
        out_shape=jax.ShapeDtypeStruct((rows, width), jnp.float32),
        cost_estimate=pl.CostEstimate(
            flops=flops,
            transcendentals=rows * 2 * kv_rows * H,
            bytes_accessed=4 * kv_rows * 1024 + rows * width * 10,
        ),
    )(mult, tiers, qpos, kpos_a, kpos_b, queries, block_a, block_a, block_b, block_b, x, w_out)


def local(
    residual_flow,
    tiers_each_segment,
    resident_tile_order,
    normalizer_weight_entries,
    lookup_map_weights,
    content_map_weights,
    softmax_warmth,
    attention_result_weight,
):
    tok_rows = residual_flow.shape[1]
    n_ctx = lax.axis_size("ctx")
    n_chips = n_ctx // 2
    me = lax.axis_index("ctx")
    core = me % 2
    chip = me // 2
    half_rows = tok_rows // 2
    residual = residual_flow[0]

    all_pos = (
        jnp.repeat(resident_tile_order.astype(jnp.int32), half_rows) * half_rows
        + jnp.tile(jnp.arange(half_rows, dtype=jnp.int32), resident_tile_order.shape[0])
    )
    query_pos = lax.dynamic_slice(all_pos, (me * tok_rows,), (tok_rows,)).reshape(tok_rows, 1)
    by_part = all_pos.reshape(n_chips, 2, 2, half_rows)
    behind = (chip - jnp.arange(n_chips, dtype=jnp.int32)) % n_chips

    def key_positions(of_core):
        rows = lax.dynamic_index_in_dim(by_part, of_core, axis=1, keepdims=False)
        first = rows[:, 0, :].reshape(-1)
        second = jnp.take(rows[:, 1, :], behind, axis=0).reshape(-1)
        return jnp.concatenate([first, second]).reshape(1, -1)

    pos_mine = key_positions(core)
    pos_theirs = key_positions(1 - core)

    own_block, queries = prologue(
        residual,
        normalizer_weight_entries[0],
        lookup_map_weights[0, 0],
        content_map_weights[0, 0],
    )
    mult = softmax_warmth[0, 0] / ATTN_UNIT_WIDTH
    own_block, queries, query_pos, pos_mine, pos_theirs, mult = lax.optimization_barrier(
        (own_block, queries, query_pos, pos_mine, pos_theirs, mult)
    )

    same_core = [list(range(c, n_ctx, 2)) for c in range(2)]
    partner_route = [(i, i ^ 1) for i in range(n_ctx)]
    first_half = lax.all_gather(
        own_block[:half_rows], "ctx", axis=0, tiled=True, axis_index_groups=same_core
    )
    second_halves = [own_block[half_rows:]]
    for distance in range(1, n_chips):
        route = [(i, ((i // 2 + distance) % n_chips) * 2 + i % 2) for i in range(n_ctx)]
        second_halves.append(lax.ppermute(own_block[half_rows:], "ctx", route))
    mine = jnp.concatenate([first_half] + second_halves, axis=0)
    theirs = lax.ppermute(mine, "ctx", partner_route)

    residual = attend_and_update(
        mult,
        tiers_each_segment,
        query_pos,
        pos_mine,
        pos_theirs,
        queries,
        mine,
        theirs,
        residual,
        attention_result_weight[0],
    )
    return passed_along(residual[None], "section", 1)


def solution(mesh):
    in_specs = (
        P("section", "ctx", None),
        P("section"),
        P(),
        P("section", None, None),
        P("section", None, None, None),
        P("section", None, None, None),
        P("section", None, None),
        P("section", None, None),
    )
    out_specs = P("section", "ctx", None)
    return jax.shard_map(local, mesh=mesh, in_specs=in_specs, out_specs=out_specs, check_vma=False)
```

```python
import functools

import jax
import jax.numpy as jnp
from jax import lax
from jax.experimental import pallas as pl
from jax.experimental.pallas import tpu as pltpu
from jax.sharding import PartitionSpec as P

H = 16
KEY_VALUE_HEADS = 4
ATTN_UNIT_WIDTH = 128


def passed_along(block, axis, distance):
    devices = range(lax.axis_size(axis))
    route = [((i - distance) % len(devices), i) for i in devices]
    return lax.ppermute(block, axis, route)


def head_norm(values):
    return values * lax.rsqrt(jnp.mean(values * values, axis=-1, keepdims=True) + 1e-05)


def attention_kernel(
    mult_ref, tiers_ref, qpos_ref, kpos_a_ref, kpos_b_ref, q_ref,
    ka_ref, va_ref, kb_ref, vb_ref, w_ref, out_ref,
):
    c = pl.program_id(0)
    group = q_ref.shape[1] // ATTN_UNIT_WIDTH
    qpos = qpos_ref[...]
    allowed_a = kpos_a_ref[...] <= qpos
    allowed_b = kpos_b_ref[...] <= qpos
    ka = ka_ref[...]
    kb = kb_ref[...]
    va = va_ref[...]
    vb = vb_ref[...]
    gate = tiers_ref[0] > 0
    dims = (((1,), (1,)), ((), ()))
    for g in range(group):
        cols = slice(g * ATTN_UNIT_WIDTH, (g + 1) * ATTN_UNIT_WIDTH)
        qh = q_ref[:, cols]
        mult = mult_ref[c * group + g]
        s_a = jnp.where(allowed_a, lax.dot_general(qh, ka, dims, preferred_element_type=jnp.float32), -1e30)
        s_b = jnp.where(allowed_b, lax.dot_general(qh, kb, dims, preferred_element_type=jnp.float32), -1e30)
        row_max = jnp.maximum(
            jnp.max(s_a, axis=1, keepdims=True), jnp.max(s_b, axis=1, keepdims=True)
        ) * mult
        p_a = jnp.exp(s_a * mult - row_max)
        p_b = jnp.exp(s_b * mult - row_max)
        total = jnp.sum(p_a, axis=1, keepdims=True) + jnp.sum(p_b, axis=1, keepdims=True)
        mixed = jnp.dot(
            p_a.astype(jnp.bfloat16), va, preferred_element_type=jnp.float32
        ) + jnp.dot(p_b.astype(jnp.bfloat16), vb, preferred_element_type=jnp.float32)
        mixed = mixed / total
        out_ref[:, cols] = jnp.where(gate, w_ref[:, cols] * mixed, 0.0).astype(out_ref.dtype)


def prologue_kernel(x_ref, gain_ref, wk_ref, wv_ref, kv_ref, q_ref):
    x = x_ref[...]
    normed = (
        x * lax.rsqrt(jnp.mean(x * x, axis=1, keepdims=True) + 1e-05) * gain_ref[...]
    ).astype(jnp.bfloat16)
    keys = jnp.dot(normed, wk_ref[...], preferred_element_type=jnp.float32)
    kv_cols = keys.shape[1]
    for c in range(kv_cols // ATTN_UNIT_WIDTH):
        cols = slice(c * ATTN_UNIT_WIDTH, (c + 1) * ATTN_UNIT_WIDTH)
        kv_ref[:, cols] = head_norm(keys[:, cols]).astype(jnp.bfloat16)
    kv_ref[:, kv_cols:] = jnp.dot(
        normed, wv_ref[...], preferred_element_type=jnp.float32
    ).astype(jnp.bfloat16)
    wide = normed.astype(jnp.float32)
    for h in range(wide.shape[1] // ATTN_UNIT_WIDTH):
        cols = slice(h * ATTN_UNIT_WIDTH, (h + 1) * ATTN_UNIT_WIDTH)
        q_ref[:, cols] = head_norm(wide[:, cols]).astype(jnp.bfloat16)


def prologue(x, gain, wk, wv):
    rows, width = x.shape
    kv_cols = wk.shape[1]
    return pl.pallas_call(
        prologue_kernel,
        out_shape=(
            jax.ShapeDtypeStruct((rows, 2 * kv_cols), jnp.bfloat16),
            jax.ShapeDtypeStruct((rows, width), jnp.bfloat16),
        ),
        cost_estimate=pl.CostEstimate(
            flops=4 * rows * width * kv_cols,
            transcendentals=rows * 24,
            bytes_accessed=2 * width * kv_cols * 2 + rows * width * 6 + rows * kv_cols * 4,
        ),
    )(x, gain, wk, wv)


def attend_and_update(mult, tiers, qpos, kpos_a, kpos_b, queries, block_a, block_b, w_out):
    rows, width = queries.shape
    kv_rows = block_a.shape[0]
    kv_heads = KEY_VALUE_HEADS
    head_cols = width // kv_heads
    smem = pl.BlockSpec(memory_space=pltpu.SMEM)
    whole = lambda shape: pl.BlockSpec(shape, lambda c: (0, 0))
    cols = lambda shape: pl.BlockSpec(shape, lambda c: (0, c))
    values_at = lambda shape: pl.BlockSpec(shape, lambda c: (0, c + kv_heads))
    kv_block = (kv_rows, ATTN_UNIT_WIDTH)
    flops = 4 * rows * 2 * kv_rows * ATTN_UNIT_WIDTH * H
    return pl.pallas_call(
        attention_kernel,
        grid=(kv_heads,),
        in_specs=[
            smem,
            smem,
            whole((rows, 1)),
            whole((1, kv_rows)),
            whole((1, kv_rows)),
            cols((rows, head_cols)),
            cols(kv_block),
            values_at(kv_block),
            cols(kv_block),
            values_at(kv_block),
            cols((1, head_cols)),
        ],
        out_specs=cols((rows, head_cols)),
        out_shape=jax.ShapeDtypeStruct((rows, width), jnp.float32),
        cost_estimate=pl.CostEstimate(
            flops=flops,
            transcendentals=rows * 2 * kv_rows * H,
            bytes_accessed=4 * kv_rows * 1024 + rows * width * 10,
        ),
    )(mult, tiers, qpos, kpos_a, kpos_b, queries, block_a, block_a, block_b, block_b, w_out)


def local(
    residual_flow,
    tiers_each_segment,
    resident_tile_order,
    normalizer_weight_entries,
    lookup_map_weights,
    content_map_weights,
    softmax_warmth,
    attention_result_weight,
):
    tok_rows = residual_flow.shape[1]
    n_ctx = lax.axis_size("ctx")
    n_chips = n_ctx // 2
    me = lax.axis_index("ctx")
    core = me % 2
    half_rows = tok_rows // 2
    residual = residual_flow[0]
    residual_next = passed_along(residual_flow, "section", 1)

    all_pos = (
        jnp.repeat(resident_tile_order.astype(jnp.int32), half_rows) * half_rows
        + jnp.tile(jnp.arange(half_rows, dtype=jnp.int32), resident_tile_order.shape[0])
    )
    query_pos = lax.dynamic_slice(all_pos, (me * tok_rows,), (tok_rows,)).reshape(tok_rows, 1)
    by_core = all_pos.reshape(n_chips, 2, tok_rows)
    pos_mine = lax.dynamic_index_in_dim(by_core, core, axis=1, keepdims=False).reshape(1, -1)
    pos_theirs = lax.dynamic_index_in_dim(by_core, 1 - core, axis=1, keepdims=False).reshape(1, -1)

    own_block, queries = prologue(
        residual,
        normalizer_weight_entries[0],
        lookup_map_weights[0, 0],
        content_map_weights[0, 0],
    )
    mult = softmax_warmth[0, 0] / ATTN_UNIT_WIDTH
    own_block, queries, query_pos, pos_mine, pos_theirs, mult = lax.optimization_barrier(
        (own_block, queries, query_pos, pos_mine, pos_theirs, mult)
    )

    same_core = [list(range(c, n_ctx, 2)) for c in range(2)]
    partner_route = [(i, i ^ 1) for i in range(n_ctx)]
    mine = lax.all_gather(own_block, "ctx", axis=0, tiled=True, axis_index_groups=same_core)
    mine, residual_next = lax.optimization_barrier((mine, residual_next))
    theirs = lax.ppermute(mine, "ctx", partner_route)

    update = attend_and_update(
        mult,
        tiers_each_segment,
        query_pos,
        pos_mine,
        pos_theirs,
        queries,
        mine,
        theirs,
        attention_result_weight[0],
    )
    update = update.astype(jnp.float16)
    return residual_next + passed_along(update[None], "section", 1).astype(jnp.float32)


def solution(mesh):
    in_specs = (
        P("section", "ctx", None),
        P("section"),
        P(),
        P("section", None, None),
        P("section", None, None, None),
        P("section", None, None, None),
        P("section", None, None),
        P("section", None, None),
    )
    out_specs = P("section", "ctx", None)
    return jax.shard_map(local, mesh=mesh, in_specs=in_specs, out_specs=out_specs, check_vma=False)
```

```python
import functools

import jax
import jax.numpy as jnp
from jax import lax
from jax.experimental import pallas as pl
from jax.experimental.pallas import tpu as pltpu
from jax.sharding import PartitionSpec as P

H = 16
KEY_VALUE_HEADS = 4
ATTN_UNIT_WIDTH = 128


def passed_along(block, axis, distance):
    devices = range(lax.axis_size(axis))
    route = [((i - distance) % len(devices), i) for i in devices]
    return lax.ppermute(block, axis, route)


def head_norm(values):
    return values * lax.rsqrt(jnp.mean(values * values, axis=-1, keepdims=True) + 1e-05)


def attention_kernel(
    warmth_ref, tiers_ref, order_ref, me_ref, q_ref,
    ka_ref, va_ref, kb_ref, vb_ref, w_ref, out_ref,
):
    c = pl.program_id(0)
    group = q_ref.shape[1] // ATTN_UNIT_WIDTH
    rows = q_ref.shape[0]
    half = rows // 2
    kv_rows = ka_ref.shape[0]
    me = me_ref[0]
    core = me % 2
    r = lax.broadcasted_iota(jnp.int32, (rows, 1), 0)
    qpos = jnp.where(
        r < half, order_ref[2 * me] * half + r, order_ref[2 * me + 1] * half + r - half
    )
    j = lax.broadcasted_iota(jnp.int32, (1, kv_rows), 1)
    tile = j // half
    offset = j % half

    def key_positions(of_core):
        pos = offset
        for t in range(kv_rows // half):
            block = 4 * (t // 2) + 2 * of_core + t % 2
            pos = pos + jnp.where(tile == t, order_ref[block] * half, 0)
        return pos

    allowed_a = key_positions(core) <= qpos
    allowed_b = key_positions(1 - core) <= qpos
    ka = ka_ref[...]
    kb = kb_ref[...]
    va = va_ref[...]
    vb = vb_ref[...]
    gate = tiers_ref[0] > 0
    dims = (((1,), (1,)), ((), ()))
    for g in range(group):
        cols = slice(g * ATTN_UNIT_WIDTH, (g + 1) * ATTN_UNIT_WIDTH)
        qh = q_ref[:, cols]
        mult = warmth_ref[c * group + g] * (1.0 / ATTN_UNIT_WIDTH)
        s_a = jnp.where(allowed_a, lax.dot_general(qh, ka, dims, preferred_element_type=jnp.float32), -1e30)
        s_b = jnp.where(allowed_b, lax.dot_general(qh, kb, dims, preferred_element_type=jnp.float32), -1e30)
        row_max = jnp.maximum(
            jnp.max(s_a, axis=1, keepdims=True), jnp.max(s_b, axis=1, keepdims=True)
        ) * mult
        p_a = jnp.exp(s_a * mult - row_max)
        p_b = jnp.exp(s_b * mult - row_max)
        total = jnp.sum(p_a, axis=1, keepdims=True) + jnp.sum(p_b, axis=1, keepdims=True)
        mixed = jnp.dot(
            p_a.astype(jnp.bfloat16), va, preferred_element_type=jnp.float32
        ) + jnp.dot(p_b.astype(jnp.bfloat16), vb, preferred_element_type=jnp.float32)
        mixed = mixed / total
        out_ref[:, cols] = jnp.where(gate, w_ref[:, cols] * mixed, 0.0).astype(out_ref.dtype)


def prologue_kernel(x_ref, gain_ref, wk_ref, wv_ref, kv_ref, q_ref):
    x = x_ref[...]
    normed = (
        x * lax.rsqrt(jnp.mean(x * x, axis=1, keepdims=True) + 1e-05) * gain_ref[...]
    ).astype(jnp.bfloat16)
    keys = jnp.dot(normed, wk_ref[...], preferred_element_type=jnp.float32)
    kv_cols = keys.shape[1]
    for c in range(kv_cols // ATTN_UNIT_WIDTH):
        cols = slice(c * ATTN_UNIT_WIDTH, (c + 1) * ATTN_UNIT_WIDTH)
        kv_ref[:, cols] = head_norm(keys[:, cols]).astype(jnp.bfloat16)
    kv_ref[:, kv_cols:] = jnp.dot(
        normed, wv_ref[...], preferred_element_type=jnp.float32
    ).astype(jnp.bfloat16)
    wide = normed.astype(jnp.float32)
    for h in range(wide.shape[1] // ATTN_UNIT_WIDTH):
        cols = slice(h * ATTN_UNIT_WIDTH, (h + 1) * ATTN_UNIT_WIDTH)
        q_ref[:, cols] = head_norm(wide[:, cols]).astype(jnp.bfloat16)


def prologue(x, gain, wk, wv):
    rows, width = x.shape
    kv_cols = wk.shape[1]
    return pl.pallas_call(
        prologue_kernel,
        out_shape=(
            jax.ShapeDtypeStruct((rows, 2 * kv_cols), jnp.bfloat16),
            jax.ShapeDtypeStruct((rows, width), jnp.bfloat16),
        ),
        cost_estimate=pl.CostEstimate(
            flops=4 * rows * width * kv_cols,
            transcendentals=rows * 24,
            bytes_accessed=2 * width * kv_cols * 2 + rows * width * 6 + rows * kv_cols * 4,
        ),
    )(x, gain, wk, wv)


def attend_and_update(warmth, tiers, order, me, queries, block_a, block_b, w_out):
    rows, width = queries.shape
    kv_rows = block_a.shape[0]
    kv_heads = KEY_VALUE_HEADS
    head_cols = width // kv_heads
    smem = pl.BlockSpec(memory_space=pltpu.SMEM)
    whole = lambda shape: pl.BlockSpec(shape, lambda c: (0, 0))
    cols = lambda shape: pl.BlockSpec(shape, lambda c: (0, c))
    values_at = lambda shape: pl.BlockSpec(shape, lambda c: (0, c + kv_heads))
    kv_block = (kv_rows, ATTN_UNIT_WIDTH)
    flops = 4 * rows * 2 * kv_rows * ATTN_UNIT_WIDTH * H
    return pl.pallas_call(
        attention_kernel,
        grid=(kv_heads,),
        in_specs=[
            smem,
            smem,
            smem,
            smem,
            cols((rows, head_cols)),
            cols(kv_block),
            values_at(kv_block),
            cols(kv_block),
            values_at(kv_block),
            cols((1, head_cols)),
        ],
        out_specs=cols((rows, head_cols)),
        out_shape=jax.ShapeDtypeStruct((rows, width), jnp.float32),
        cost_estimate=pl.CostEstimate(
            flops=flops,
            transcendentals=rows * 2 * kv_rows * H,
            bytes_accessed=4 * kv_rows * 1024 + rows * width * 10,
        ),
    )(warmth, tiers, order, me, queries, block_a, block_a, block_b, block_b, w_out)


def local(
    residual_flow,
    tiers_each_segment,
    resident_tile_order,
    normalizer_weight_entries,
    lookup_map_weights,
    content_map_weights,
    softmax_warmth,
    attention_result_weight,
):
    tok_rows = residual_flow.shape[1]
    n_ctx = lax.axis_size("ctx")
    n_chips = n_ctx // 2
    me = lax.axis_index("ctx")
    core = me % 2
    half_rows = tok_rows // 2
    residual = residual_flow[0]
    residual_next = passed_along(residual_flow, "section", 1)

    own_block, queries = prologue(
        residual,
        normalizer_weight_entries[0],
        lookup_map_weights[0, 0],
        content_map_weights[0, 0],
    )
    own_block, queries = lax.optimization_barrier((own_block, queries))

    same_core = [list(range(c, n_ctx, 2)) for c in range(2)]
    partner_route = [(i, i ^ 1) for i in range(n_ctx)]
    mine = lax.all_gather(own_block, "ctx", axis=0, tiled=True, axis_index_groups=same_core)
    mine, residual_next = lax.optimization_barrier((mine, residual_next))
    theirs = lax.ppermute(mine, "ctx", partner_route)

    update = attend_and_update(
        softmax_warmth[0, 0],
        tiers_each_segment,
        resident_tile_order,
        me.reshape(1).astype(jnp.int32),
        queries,
        mine,
        theirs,
        attention_result_weight[0],
    )
    update = update.astype(jnp.float16)
    return residual_next + passed_along(update[None], "section", 1).astype(jnp.float32)


def solution(mesh):
    in_specs = (
        P("section", "ctx", None),
        P("section"),
        P(),
        P("section", None, None),
        P("section", None, None, None),
        P("section", None, None, None),
        P("section", None, None),
        P("section", None, None),
    )
    out_specs = P("section", "ctx", None)
    return jax.shard_map(local, mesh=mesh, in_specs=in_specs, out_specs=out_specs, check_vma=False)
```

```python
import functools

import jax
import jax.numpy as jnp
from jax import lax
from jax.experimental import pallas as pl
from jax.experimental.pallas import tpu as pltpu
from jax.sharding import PartitionSpec as P

H = 16
KEY_VALUE_HEADS = 4
ATTN_UNIT_WIDTH = 128


def passed_along(block, axis, distance):
    devices = range(lax.axis_size(axis))
    route = [((i - distance) % len(devices), i) for i in devices]
    return lax.ppermute(block, axis, route)


def head_norm(values):
    return values * lax.rsqrt(jnp.mean(values * values, axis=-1, keepdims=True) + 1e-05)


def attention_kernel(
    warmth_ref, tiers_ref, order_ref, me_ref, q_ref,
    ka_ref, va_ref, kb_ref, vb_ref, w_ref, out_ref,
):
    c = pl.program_id(0)
    group = q_ref.shape[1] // ATTN_UNIT_WIDTH
    rows = q_ref.shape[0]
    half = rows // 2
    kv_rows = ka_ref.shape[0]
    me = me_ref[0]
    core = me % 2
    r = lax.broadcasted_iota(jnp.int32, (rows, 1), 0)
    qpos = jnp.where(
        r < half, order_ref[2 * me] * half + r, order_ref[2 * me + 1] * half + r - half
    )
    j = lax.broadcasted_iota(jnp.int32, (1, kv_rows), 1)
    tile = j // half
    offset = j % half

    def key_positions(of_core):
        pos = offset
        for t in range(kv_rows // half):
            block = 4 * (t // 2) + 2 * of_core + t % 2
            pos = pos + jnp.where(tile == t, order_ref[block] * half, 0)
        return pos

    allowed_a = key_positions(core) <= qpos
    allowed_b = key_positions(1 - core) <= qpos
    ka = ka_ref[...]
    kb = kb_ref[...]
    va = va_ref[...]
    vb = vb_ref[...]
    gate = tiers_ref[0] > 0
    dims = (((1,), (1,)), ((), ()))
    for g in range(group):
        cols = slice(g * ATTN_UNIT_WIDTH, (g + 1) * ATTN_UNIT_WIDTH)
        qh = q_ref[:, cols]
        mult = warmth_ref[c * group + g] * (1.0 / ATTN_UNIT_WIDTH)
        s_a = jnp.where(allowed_a, lax.dot_general(qh, ka, dims, preferred_element_type=jnp.float32), -1e30)
        s_b = jnp.where(allowed_b, lax.dot_general(qh, kb, dims, preferred_element_type=jnp.float32), -1e30)
        row_max = jnp.maximum(
            jnp.max(s_a, axis=1, keepdims=True), jnp.max(s_b, axis=1, keepdims=True)
        ) * mult
        p_a = jnp.exp(s_a * mult - row_max)
        p_b = jnp.exp(s_b * mult - row_max)
        total = jnp.sum(p_a, axis=1, keepdims=True) + jnp.sum(p_b, axis=1, keepdims=True)
        mixed = jnp.dot(
            p_a.astype(jnp.bfloat16), va, preferred_element_type=jnp.float32
        ) + jnp.dot(p_b.astype(jnp.bfloat16), vb, preferred_element_type=jnp.float32)
        mixed = mixed / total
        out_ref[:, cols] = jnp.where(gate, w_ref[:, cols] * mixed, 0.0).astype(out_ref.dtype)


def normed_rows(x_ref, gain_ref):
    x = x_ref[...]
    return (
        x * lax.rsqrt(jnp.mean(x * x, axis=1, keepdims=True) + 1e-05) * gain_ref[...]
    ).astype(jnp.bfloat16)


def key_value_kernel(x_ref, gain_ref, wk_ref, wv_ref, kv_ref):
    normed = normed_rows(x_ref, gain_ref)
    keys = jnp.dot(normed, wk_ref[...], preferred_element_type=jnp.float32)
    kv_cols = keys.shape[1]
    for c in range(kv_cols // ATTN_UNIT_WIDTH):
        cols = slice(c * ATTN_UNIT_WIDTH, (c + 1) * ATTN_UNIT_WIDTH)
        kv_ref[:, cols] = head_norm(keys[:, cols]).astype(jnp.bfloat16)
    kv_ref[:, kv_cols:] = jnp.dot(
        normed, wv_ref[...], preferred_element_type=jnp.float32
    ).astype(jnp.bfloat16)


def query_kernel(x_ref, gain_ref, q_ref):
    wide = normed_rows(x_ref, gain_ref).astype(jnp.float32)
    for h in range(wide.shape[1] // ATTN_UNIT_WIDTH):
        cols = slice(h * ATTN_UNIT_WIDTH, (h + 1) * ATTN_UNIT_WIDTH)
        q_ref[:, cols] = head_norm(wide[:, cols]).astype(jnp.bfloat16)


def prologue(x, gain, wk, wv):
    rows, width = x.shape
    kv_cols = wk.shape[1]
    own_block = pl.pallas_call(
        key_value_kernel,
        out_shape=jax.ShapeDtypeStruct((rows, 2 * kv_cols), jnp.bfloat16),
        cost_estimate=pl.CostEstimate(
            flops=4 * rows * width * kv_cols,
            transcendentals=rows * 8,
            bytes_accessed=2 * width * kv_cols * 2 + rows * width * 4 + rows * kv_cols * 4,
        ),
    )(x, gain, wk, wv)
    queries = pl.pallas_call(
        query_kernel,
        out_shape=jax.ShapeDtypeStruct((rows, width), jnp.bfloat16),
        cost_estimate=pl.CostEstimate(
            flops=8 * rows * width, transcendentals=rows * 20, bytes_accessed=rows * width * 6
        ),
    )(x, gain)
    return own_block, queries


def attend_and_update(warmth, tiers, order, me, queries, block_a, block_b, w_out):
    rows, width = queries.shape
    kv_rows = block_a.shape[0]
    kv_heads = KEY_VALUE_HEADS
    head_cols = width // kv_heads
    smem = pl.BlockSpec(memory_space=pltpu.SMEM)
    whole = lambda shape: pl.BlockSpec(shape, lambda c: (0, 0))
    cols = lambda shape: pl.BlockSpec(shape, lambda c: (0, c))
    values_at = lambda shape: pl.BlockSpec(shape, lambda c: (0, c + kv_heads))
    kv_block = (kv_rows, ATTN_UNIT_WIDTH)
    flops = 4 * rows * 2 * kv_rows * ATTN_UNIT_WIDTH * H
    return pl.pallas_call(
        attention_kernel,
        grid=(kv_heads,),
        in_specs=[
            smem,
            smem,
            smem,
            smem,
            cols((rows, head_cols)),
            cols(kv_block),
            values_at(kv_block),
            cols(kv_block),
            values_at(kv_block),
            cols((1, head_cols)),
        ],
        out_specs=cols((rows, head_cols)),
        out_shape=jax.ShapeDtypeStruct((rows, width), jnp.float32),
        cost_estimate=pl.CostEstimate(
            flops=flops,
            transcendentals=rows * 2 * kv_rows * H,
            bytes_accessed=4 * kv_rows * 1024 + rows * width * 10,
        ),
    )(warmth, tiers, order, me, queries, block_a, block_a, block_b, block_b, w_out)


def local(
    residual_flow,
    tiers_each_segment,
    resident_tile_order,
    normalizer_weight_entries,
    lookup_map_weights,
    content_map_weights,
    softmax_warmth,
    attention_result_weight,
):
    tok_rows = residual_flow.shape[1]
    n_ctx = lax.axis_size("ctx")
    n_chips = n_ctx // 2
    me = lax.axis_index("ctx")
    core = me % 2
    half_rows = tok_rows // 2
    residual = residual_flow[0]
    residual_next = passed_along(residual_flow, "section", 1)

    own_block, queries = prologue(
        residual,
        normalizer_weight_entries[0],
        lookup_map_weights[0, 0],
        content_map_weights[0, 0],
    )
    own_block = lax.optimization_barrier(own_block)

    same_core = [list(range(c, n_ctx, 2)) for c in range(2)]
    partner_route = [(i, i ^ 1) for i in range(n_ctx)]
    mine = lax.all_gather(own_block, "ctx", axis=0, tiled=True, axis_index_groups=same_core)
    mine, residual_next, queries = lax.optimization_barrier((mine, residual_next, queries))
    theirs = lax.ppermute(mine, "ctx", partner_route)

    update = attend_and_update(
        softmax_warmth[0, 0],
        tiers_each_segment,
        resident_tile_order,
        me.reshape(1).astype(jnp.int32),
        queries,
        mine,
        theirs,
        attention_result_weight[0],
    )
    update = update.astype(jnp.float16)
    return residual_next + passed_along(update[None], "section", 1).astype(jnp.float32)


def solution(mesh):
    in_specs = (
        P("section", "ctx", None),
        P("section"),
        P(),
        P("section", None, None),
        P("section", None, None, None),
        P("section", None, None, None),
        P("section", None, None),
        P("section", None, None),
    )
    out_specs = P("section", "ctx", None)
    return jax.shard_map(local, mesh=mesh, in_specs=in_specs, out_specs=out_specs, check_vma=False)
```

```python
import functools

import jax
import jax.numpy as jnp
from jax import lax
from jax.experimental import pallas as pl
from jax.experimental.pallas import tpu as pltpu
from jax.sharding import PartitionSpec as P

H = 16
KEY_VALUE_HEADS = 4
ATTN_UNIT_WIDTH = 128


def passed_along(block, axis, distance):
    devices = range(lax.axis_size(axis))
    route = [((i - distance) % len(devices), i) for i in devices]
    return lax.ppermute(block, axis, route)


def head_norm(values):
    return values * lax.rsqrt(jnp.mean(values * values, axis=-1, keepdims=True) + 1e-05)


def attention_kernel(
    warmth_ref, tiers_ref, order_ref, me_ref, q_ref,
    ka_ref, va_ref, kb_ref, vb_ref, w_ref, out_ref,
):
    c = pl.program_id(0)
    group = q_ref.shape[1] // ATTN_UNIT_WIDTH
    rows = q_ref.shape[0]
    half = rows // 2
    kv_rows = ka_ref.shape[0]
    me = me_ref[0]
    r = lax.broadcasted_iota(jnp.int32, (rows, 1), 0)
    qpos = jnp.where(
        r < half, order_ref[2 * me] * half + r, order_ref[2 * me + 1] * half + r - half
    )
    j = lax.broadcasted_iota(jnp.int32, (1, kv_rows), 1)
    tile = j // half
    offset = j % half

    def key_positions(first_block):
        pos = offset
        for t in range(kv_rows // half):
            pos = pos + jnp.where(tile == t, order_ref[first_block + t] * half, 0)
        return pos

    allowed_a = key_positions(0) <= qpos
    allowed_b = key_positions(kv_rows // half) <= qpos
    ka = ka_ref[...]
    kb = kb_ref[...]
    va = va_ref[...]
    vb = vb_ref[...]
    gate = tiers_ref[0] > 0
    dims = (((1,), (1,)), ((), ()))
    for g in range(group):
        cols = slice(g * ATTN_UNIT_WIDTH, (g + 1) * ATTN_UNIT_WIDTH)
        qh = q_ref[:, cols]
        mult = warmth_ref[c * group + g] * (1.0 / ATTN_UNIT_WIDTH)
        s_a = jnp.where(allowed_a, lax.dot_general(qh, ka, dims, preferred_element_type=jnp.float32), -1e30)
        s_b = jnp.where(allowed_b, lax.dot_general(qh, kb, dims, preferred_element_type=jnp.float32), -1e30)
        row_max = jnp.maximum(
            jnp.max(s_a, axis=1, keepdims=True), jnp.max(s_b, axis=1, keepdims=True)
        ) * mult
        p_a = jnp.exp(s_a * mult - row_max)
        p_b = jnp.exp(s_b * mult - row_max)
        total = jnp.sum(p_a, axis=1, keepdims=True) + jnp.sum(p_b, axis=1, keepdims=True)
        mixed = jnp.dot(
            p_a.astype(jnp.bfloat16), va, preferred_element_type=jnp.float32
        ) + jnp.dot(p_b.astype(jnp.bfloat16), vb, preferred_element_type=jnp.float32)
        mixed = mixed / total
        out_ref[:, cols] = jnp.where(gate, w_ref[:, cols] * mixed, 0.0).astype(out_ref.dtype)


def normed_rows(x_ref, gain_ref):
    x = x_ref[...]
    return (
        x * lax.rsqrt(jnp.mean(x * x, axis=1, keepdims=True) + 1e-05) * gain_ref[...]
    ).astype(jnp.bfloat16)


def key_value_kernel(x_ref, gain_ref, wk_ref, wv_ref, kv_ref):
    normed = normed_rows(x_ref, gain_ref)
    keys = jnp.dot(normed, wk_ref[...], preferred_element_type=jnp.float32)
    kv_cols = keys.shape[1]
    for c in range(kv_cols // ATTN_UNIT_WIDTH):
        cols = slice(c * ATTN_UNIT_WIDTH, (c + 1) * ATTN_UNIT_WIDTH)
        kv_ref[:, cols] = head_norm(keys[:, cols]).astype(jnp.bfloat16)
    kv_ref[:, kv_cols:] = jnp.dot(
        normed, wv_ref[...], preferred_element_type=jnp.float32
    ).astype(jnp.bfloat16)


def query_kernel(x_ref, gain_ref, q_ref):
    wide = normed_rows(x_ref, gain_ref).astype(jnp.float32)
    for h in range(wide.shape[1] // ATTN_UNIT_WIDTH):
        cols = slice(h * ATTN_UNIT_WIDTH, (h + 1) * ATTN_UNIT_WIDTH)
        q_ref[:, cols] = head_norm(wide[:, cols]).astype(jnp.bfloat16)


def prologue(x, gain, wk, wv):
    rows, width = x.shape
    kv_cols = wk.shape[1]
    own_block = pl.pallas_call(
        key_value_kernel,
        out_shape=jax.ShapeDtypeStruct((rows, 2 * kv_cols), jnp.bfloat16),
        cost_estimate=pl.CostEstimate(
            flops=4 * rows * width * kv_cols,
            transcendentals=rows * 8,
            bytes_accessed=2 * width * kv_cols * 2 + rows * width * 4 + rows * kv_cols * 4,
        ),
    )(x, gain, wk, wv)
    queries = pl.pallas_call(
        query_kernel,
        out_shape=jax.ShapeDtypeStruct((rows, width), jnp.bfloat16),
        cost_estimate=pl.CostEstimate(
            flops=8 * rows * width, transcendentals=rows * 20, bytes_accessed=rows * width * 6
        ),
    )(x, gain)
    return own_block, queries


def attend_and_update(warmth, tiers, order, me, queries, block_a, block_b, w_out):
    rows, width = queries.shape
    kv_rows = block_a.shape[0]
    kv_heads = KEY_VALUE_HEADS
    head_cols = width // kv_heads
    smem = pl.BlockSpec(memory_space=pltpu.SMEM)
    whole = lambda shape: pl.BlockSpec(shape, lambda c: (0, 0))
    cols = lambda shape: pl.BlockSpec(shape, lambda c: (0, c))
    values_at = lambda shape: pl.BlockSpec(shape, lambda c: (0, c + kv_heads))
    kv_block = (kv_rows, ATTN_UNIT_WIDTH)
    flops = 4 * rows * 2 * kv_rows * ATTN_UNIT_WIDTH * H
    return pl.pallas_call(
        attention_kernel,
        grid=(kv_heads,),
        in_specs=[
            smem,
            smem,
            smem,
            smem,
            cols((rows, head_cols)),
            cols(kv_block),
            values_at(kv_block),
            cols(kv_block),
            values_at(kv_block),
            cols((1, head_cols)),
        ],
        out_specs=cols((rows, head_cols)),
        out_shape=jax.ShapeDtypeStruct((rows, width), jnp.float32),
        cost_estimate=pl.CostEstimate(
            flops=flops,
            transcendentals=rows * 2 * kv_rows * H,
            bytes_accessed=4 * kv_rows * 1024 + rows * width * 10,
        ),
    )(warmth, tiers, order, me, queries, block_a, block_a, block_b, block_b, w_out)


def local(
    residual_flow,
    tiers_each_segment,
    resident_tile_order,
    normalizer_weight_entries,
    lookup_map_weights,
    content_map_weights,
    softmax_warmth,
    attention_result_weight,
):
    tok_rows = residual_flow.shape[1]
    n_ctx = lax.axis_size("ctx")
    n_chips = n_ctx // 2
    me = lax.axis_index("ctx")
    core = me % 2
    half_rows = tok_rows // 2
    residual = residual_flow[0]
    residual_next = passed_along(residual_flow, "section", 1)

    own_block, queries = prologue(
        residual,
        normalizer_weight_entries[0],
        lookup_map_weights[0, 0],
        content_map_weights[0, 0],
    )
    own_block = lax.optimization_barrier(own_block)

    gathered = lax.all_gather(own_block, "ctx", axis=0, tiled=True)
    gathered, residual_next, queries = lax.optimization_barrier((gathered, residual_next, queries))
    split = gathered.shape[0] // 2

    update = attend_and_update(
        softmax_warmth[0, 0],
        tiers_each_segment,
        resident_tile_order,
        me.reshape(1).astype(jnp.int32),
        queries,
        gathered[:split],
        gathered[split:],
        attention_result_weight[0],
    )
    update = update.astype(jnp.float16)
    return residual_next + passed_along(update[None], "section", 1).astype(jnp.float32)


def solution(mesh):
    in_specs = (
        P("section", "ctx", None),
        P("section"),
        P(),
        P("section", None, None),
        P("section", None, None, None),
        P("section", None, None, None),
        P("section", None, None),
        P("section", None, None),
    )
    out_specs = P("section", "ctx", None)
    return jax.shard_map(local, mesh=mesh, in_specs=in_specs, out_specs=out_specs, check_vma=False)
```

```python
import functools

import jax
import jax.numpy as jnp
from jax import lax
from jax.experimental import pallas as pl
from jax.experimental.pallas import tpu as pltpu
from jax.sharding import PartitionSpec as P

H = 16
KEY_VALUE_HEADS = 4
ATTN_UNIT_WIDTH = 128


def passed_along(block, axis, distance):
    devices = range(lax.axis_size(axis))
    route = [((i - distance) % len(devices), i) for i in devices]
    return lax.ppermute(block, axis, route)


def head_norm(values):
    return values * lax.rsqrt(jnp.mean(values * values, axis=-1, keepdims=True) + 1e-05)


def attention_kernel(
    warmth_ref, tiers_ref, order_ref, me_ref, q_ref,
    ka_ref, va_ref, kb_ref, vb_ref, w_ref, out_ref,
):
    c = pl.program_id(0)
    group = q_ref.shape[1] // ATTN_UNIT_WIDTH
    rows = q_ref.shape[0]
    half = rows // 2
    kv_rows = ka_ref.shape[0]
    me = me_ref[0]
    r = lax.broadcasted_iota(jnp.int32, (rows, 1), 0)
    qpos = jnp.where(
        r < half, order_ref[2 * me] * half + r, order_ref[2 * me + 1] * half + r - half
    )
    j = lax.broadcasted_iota(jnp.int32, (1, kv_rows), 1)
    tile = j // half
    offset = j % half

    def key_positions(first_block):
        pos = offset
        for t in range(kv_rows // half):
            pos = pos + jnp.where(tile == t, order_ref[first_block + t] * half, 0)
        return pos

    allowed_a = key_positions(0) <= qpos
    allowed_b = key_positions(kv_rows // half) <= qpos
    ka = ka_ref[...]
    kb = kb_ref[...]
    va = va_ref[...]
    vb = vb_ref[...]
    gate = tiers_ref[0] > 0
    dims = (((1,), (1,)), ((), ()))
    for g in range(group):
        cols = slice(g * ATTN_UNIT_WIDTH, (g + 1) * ATTN_UNIT_WIDTH)
        qh = q_ref[:, cols]
        mult = warmth_ref[c * group + g] * (1.0 / ATTN_UNIT_WIDTH)
        s_a = jnp.where(allowed_a, lax.dot_general(qh, ka, dims, preferred_element_type=jnp.float32), -1e30)
        s_b = jnp.where(allowed_b, lax.dot_general(qh, kb, dims, preferred_element_type=jnp.float32), -1e30)
        row_max = jnp.maximum(
            jnp.max(s_a, axis=1, keepdims=True), jnp.max(s_b, axis=1, keepdims=True)
        ) * mult
        p_a = jnp.exp(s_a * mult - row_max)
        p_b = jnp.exp(s_b * mult - row_max)
        total = jnp.sum(p_a, axis=1, keepdims=True) + jnp.sum(p_b, axis=1, keepdims=True)
        mixed = jnp.dot(
            p_a.astype(jnp.bfloat16), va, preferred_element_type=jnp.float32
        ) + jnp.dot(p_b.astype(jnp.bfloat16), vb, preferred_element_type=jnp.float32)
        mixed = mixed / total
        out_ref[:, cols] = jnp.where(gate, w_ref[:, cols] * mixed, 0.0).astype(out_ref.dtype)


def normed_rows(x_ref, gain_ref):
    x = x_ref[...]
    return (
        x * lax.rsqrt(jnp.mean(x * x, axis=1, keepdims=True) + 1e-05) * gain_ref[...]
    ).astype(jnp.bfloat16)


def key_value_kernel(x_ref, gain_ref, wk_ref, wv_ref, kv_ref):
    normed = normed_rows(x_ref, gain_ref)
    keys = jnp.dot(normed, wk_ref[...], preferred_element_type=jnp.float32)
    kv_cols = keys.shape[1]
    for c in range(kv_cols // ATTN_UNIT_WIDTH):
        cols = slice(c * ATTN_UNIT_WIDTH, (c + 1) * ATTN_UNIT_WIDTH)
        kv_ref[:, cols] = head_norm(keys[:, cols]).astype(jnp.bfloat16)
    kv_ref[:, kv_cols:] = jnp.dot(
        normed, wv_ref[...], preferred_element_type=jnp.float32
    ).astype(jnp.bfloat16)


def query_kernel(x_ref, gain_ref, q_ref):
    wide = normed_rows(x_ref, gain_ref).astype(jnp.float32)
    for h in range(wide.shape[1] // ATTN_UNIT_WIDTH):
        cols = slice(h * ATTN_UNIT_WIDTH, (h + 1) * ATTN_UNIT_WIDTH)
        q_ref[:, cols] = head_norm(wide[:, cols]).astype(jnp.bfloat16)


def prologue(x, gain, wk, wv):
    rows, width = x.shape
    kv_cols = wk.shape[1]
    own_block = pl.pallas_call(
        key_value_kernel,
        out_shape=jax.ShapeDtypeStruct((rows, 2 * kv_cols), jnp.bfloat16),
        cost_estimate=pl.CostEstimate(
            flops=4 * rows * width * kv_cols,
            transcendentals=rows * 8,
            bytes_accessed=2 * width * kv_cols * 2 + rows * width * 4 + rows * kv_cols * 4,
        ),
    )(x, gain, wk, wv)
    queries = pl.pallas_call(
        query_kernel,
        out_shape=jax.ShapeDtypeStruct((rows, width), jnp.bfloat16),
        cost_estimate=pl.CostEstimate(
            flops=8 * rows * width, transcendentals=rows * 20, bytes_accessed=rows * width * 6
        ),
    )(x, gain)
    return own_block, queries


def attend_and_update(warmth, tiers, order, me, queries, gathered, w_out):
    rows, width = queries.shape
    kv_rows = gathered.shape[0] // 2
    kv_heads = KEY_VALUE_HEADS
    head_cols = width // kv_heads
    smem = pl.BlockSpec(memory_space=pltpu.SMEM)
    whole = lambda shape: pl.BlockSpec(shape, lambda c: (0, 0))
    cols = lambda shape: pl.BlockSpec(shape, lambda c: (0, c))
    values_at = lambda shape: pl.BlockSpec(shape, lambda c: (0, c + kv_heads))
    late_keys = lambda shape: pl.BlockSpec(shape, lambda c: (1, c))
    late_values = lambda shape: pl.BlockSpec(shape, lambda c: (1, c + kv_heads))
    kv_block = (kv_rows, ATTN_UNIT_WIDTH)
    flops = 4 * rows * 2 * kv_rows * ATTN_UNIT_WIDTH * H
    return pl.pallas_call(
        attention_kernel,
        grid=(kv_heads,),
        in_specs=[
            smem,
            smem,
            smem,
            smem,
            cols((rows, head_cols)),
            cols(kv_block),
            values_at(kv_block),
            late_keys(kv_block),
            late_values(kv_block),
            cols((1, head_cols)),
        ],
        out_specs=cols((rows, head_cols)),
        out_shape=jax.ShapeDtypeStruct((rows, width), jnp.float32),
        cost_estimate=pl.CostEstimate(
            flops=flops,
            transcendentals=rows * 2 * kv_rows * H,
            bytes_accessed=4 * kv_rows * 1024 + rows * width * 10,
        ),
    )(warmth, tiers, order, me, queries, gathered, gathered, gathered, gathered, w_out)


def local(
    residual_flow,
    tiers_each_segment,
    resident_tile_order,
    normalizer_weight_entries,
    lookup_map_weights,
    content_map_weights,
    softmax_warmth,
    attention_result_weight,
):
    tok_rows = residual_flow.shape[1]
    n_ctx = lax.axis_size("ctx")
    n_chips = n_ctx // 2
    me = lax.axis_index("ctx")
    core = me % 2
    half_rows = tok_rows // 2
    residual = residual_flow[0]
    residual_next = passed_along(residual_flow, "section", 1)

    own_block, queries = prologue(
        residual,
        normalizer_weight_entries[0],
        lookup_map_weights[0, 0],
        content_map_weights[0, 0],
    )
    own_block = lax.optimization_barrier(own_block)

    gathered = lax.all_gather(own_block, "ctx", axis=0, tiled=True)
    gathered, residual_next, queries = lax.optimization_barrier((gathered, residual_next, queries))

    update = attend_and_update(
        softmax_warmth[0, 0],
        tiers_each_segment,
        resident_tile_order,
        me.reshape(1).astype(jnp.int32),
        queries,
        gathered,
        attention_result_weight[0],
    )
    update = update.astype(jnp.float16)
    return residual_next + passed_along(update[None], "section", 1).astype(jnp.float32)


def solution(mesh):
    in_specs = (
        P("section", "ctx", None),
        P("section"),
        P(),
        P("section", None, None),
        P("section", None, None, None),
        P("section", None, None, None),
        P("section", None, None),
        P("section", None, None),
    )
    out_specs = P("section", "ctx", None)
    return jax.shard_map(local, mesh=mesh, in_specs=in_specs, out_specs=out_specs, check_vma=False)
```

```python
import functools

import jax
import jax.numpy as jnp
from jax import lax
from jax.experimental import pallas as pl
from jax.experimental.pallas import tpu as pltpu
from jax.sharding import PartitionSpec as P

H = 16
KEY_VALUE_HEADS = 4
ATTN_UNIT_WIDTH = 128


def passed_along(block, axis, distance):
    devices = range(lax.axis_size(axis))
    route = [((i - distance) % len(devices), i) for i in devices]
    return lax.ppermute(block, axis, route)


def head_norm(values):
    return values * lax.rsqrt(jnp.mean(values * values, axis=-1, keepdims=True) + 1e-05)


def attention_kernel(
    warmth_ref, tiers_ref, order_ref, me_ref, q_ref,
    ka_ref, va_ref, kb_ref, vb_ref, w_ref, out_ref,
):
    c = pl.program_id(0)
    group = q_ref.shape[1] // ATTN_UNIT_WIDTH
    rows = q_ref.shape[0]
    half = rows // 2
    kv_rows = ka_ref.shape[0]
    me = me_ref[0]
    r = lax.broadcasted_iota(jnp.int32, (rows, 1), 0)
    qpos = jnp.where(
        r < half, order_ref[2 * me] * half + r, order_ref[2 * me + 1] * half + r - half
    )
    j = lax.broadcasted_iota(jnp.int32, (1, kv_rows), 1)
    tile = j // half
    offset = j % half

    def key_positions(first_block):
        pos = offset
        for t in range(kv_rows // half):
            pos = pos + jnp.where(tile == t, order_ref[first_block + t] * half, 0)
        return pos

    allowed_a = key_positions(0) <= qpos
    allowed_b = key_positions(kv_rows // half) <= qpos
    ka = ka_ref[...]
    kb = kb_ref[...]
    va = va_ref[...]
    vb = vb_ref[...]
    gate = tiers_ref[0] > 0
    dims = (((1,), (1,)), ((), ()))
    for g in range(group):
        cols = slice(g * ATTN_UNIT_WIDTH, (g + 1) * ATTN_UNIT_WIDTH)
        qh = q_ref[:, cols]
        mult = warmth_ref[c * group + g] * (1.0 / ATTN_UNIT_WIDTH)
        s_a = jnp.where(allowed_a, lax.dot_general(qh, ka, dims, preferred_element_type=jnp.float32), -1e30)
        s_b = jnp.where(allowed_b, lax.dot_general(qh, kb, dims, preferred_element_type=jnp.float32), -1e30)
        row_max = jnp.maximum(
            jnp.max(s_a, axis=1, keepdims=True), jnp.max(s_b, axis=1, keepdims=True)
        ) * mult
        p_a = jnp.exp(s_a * mult - row_max)
        p_b = jnp.exp(s_b * mult - row_max)
        total = jnp.sum(p_a, axis=1, keepdims=True) + jnp.sum(p_b, axis=1, keepdims=True)
        mixed = jnp.dot(
            p_a.astype(jnp.bfloat16), va, preferred_element_type=jnp.float32
        ) + jnp.dot(p_b.astype(jnp.bfloat16), vb, preferred_element_type=jnp.float32)
        mixed = mixed / total
        out_ref[:, cols] = jnp.where(gate, w_ref[:, cols] * mixed, 0.0).astype(out_ref.dtype)


def normed_rows(x_ref, gain_ref):
    x = x_ref[...]
    return (
        x * lax.rsqrt(jnp.mean(x * x, axis=1, keepdims=True) + 1e-05) * gain_ref[...]
    ).astype(jnp.bfloat16)


def key_value_kernel(x_ref, gain_ref, wk_ref, wv_ref, kv_ref, normed_ref, k_acc, v_acc):
    i = pl.program_id(0)
    chunks = normed_ref.shape[0]
    chunk = normed_ref.shape[2]

    @pl.when(i == 0)
    def _():
        normed = normed_rows(x_ref, gain_ref)
        for part in range(chunks):
            normed_ref[part] = normed[:, part * chunk:(part + 1) * chunk]
        k_acc[...] = jnp.zeros_like(k_acc)
        v_acc[...] = jnp.zeros_like(v_acc)

    piece = normed_ref[i]
    k_acc[...] += jnp.dot(piece, wk_ref[...], preferred_element_type=jnp.float32)
    v_acc[...] += jnp.dot(piece, wv_ref[...], preferred_element_type=jnp.float32)

    @pl.when(i == chunks - 1)
    def _():
        keys = k_acc[...]
        kv_cols = keys.shape[1]
        for c in range(kv_cols // ATTN_UNIT_WIDTH):
            cols = slice(c * ATTN_UNIT_WIDTH, (c + 1) * ATTN_UNIT_WIDTH)
            kv_ref[:, cols] = head_norm(keys[:, cols]).astype(jnp.bfloat16)
        kv_ref[:, kv_cols:] = v_acc[...].astype(jnp.bfloat16)


def query_kernel(x_ref, gain_ref, q_ref):
    wide = normed_rows(x_ref, gain_ref).astype(jnp.float32)
    for h in range(wide.shape[1] // ATTN_UNIT_WIDTH):
        cols = slice(h * ATTN_UNIT_WIDTH, (h + 1) * ATTN_UNIT_WIDTH)
        q_ref[:, cols] = head_norm(wide[:, cols]).astype(jnp.bfloat16)


def prologue(x, gain, wk, wv):
    rows, width = x.shape
    kv_cols = wk.shape[1]
    chunks = 4
    chunk = width // chunks
    own_block = pl.pallas_call(
        key_value_kernel,
        grid=(chunks,),
        in_specs=[
            pl.BlockSpec((rows, width), lambda i: (0, 0)),
            pl.BlockSpec((1, width), lambda i: (0, 0)),
            pl.BlockSpec((chunk, kv_cols), lambda i: (i, 0)),
            pl.BlockSpec((chunk, kv_cols), lambda i: (i, 0)),
        ],
        out_specs=pl.BlockSpec((rows, 2 * kv_cols), lambda i: (0, 0)),
        scratch_shapes=[
            pltpu.VMEM((chunks, rows, chunk), jnp.bfloat16),
            pltpu.VMEM((rows, kv_cols), jnp.float32),
            pltpu.VMEM((rows, kv_cols), jnp.float32),
        ],
        out_shape=jax.ShapeDtypeStruct((rows, 2 * kv_cols), jnp.bfloat16),
        cost_estimate=pl.CostEstimate(
            flops=4 * rows * width * kv_cols,
            transcendentals=rows * 8,
            bytes_accessed=2 * width * kv_cols * 2 + rows * width * 4 + rows * kv_cols * 4,
        ),
    )(x, gain, wk, wv)
    queries = pl.pallas_call(
        query_kernel,
        out_shape=jax.ShapeDtypeStruct((rows, width), jnp.bfloat16),
        cost_estimate=pl.CostEstimate(
            flops=8 * rows * width, transcendentals=rows * 20, bytes_accessed=rows * width * 6
        ),
    )(x, gain)
    return own_block, queries


def attend_and_update(warmth, tiers, order, me, queries, gathered, w_out):
    rows, width = queries.shape
    kv_rows = gathered.shape[0] // 2
    kv_heads = KEY_VALUE_HEADS
    head_cols = width // kv_heads
    smem = pl.BlockSpec(memory_space=pltpu.SMEM)
    whole = lambda shape: pl.BlockSpec(shape, lambda c: (0, 0))
    cols = lambda shape: pl.BlockSpec(shape, lambda c: (0, c))
    values_at = lambda shape: pl.BlockSpec(shape, lambda c: (0, c + kv_heads))
    late_keys = lambda shape: pl.BlockSpec(shape, lambda c: (1, c))
    late_values = lambda shape: pl.BlockSpec(shape, lambda c: (1, c + kv_heads))
    kv_block = (kv_rows, ATTN_UNIT_WIDTH)
    flops = 4 * rows * 2 * kv_rows * ATTN_UNIT_WIDTH * H
    return pl.pallas_call(
        attention_kernel,
        grid=(kv_heads,),
        in_specs=[
            smem,
            smem,
            smem,
            smem,
            cols((rows, head_cols)),
            cols(kv_block),
            values_at(kv_block),
            late_keys(kv_block),
            late_values(kv_block),
            cols((1, head_cols)),
        ],
        out_specs=cols((rows, head_cols)),
        out_shape=jax.ShapeDtypeStruct((rows, width), jnp.float32),
        cost_estimate=pl.CostEstimate(
            flops=flops,
            transcendentals=rows * 2 * kv_rows * H,
            bytes_accessed=4 * kv_rows * 1024 + rows * width * 10,
        ),
    )(warmth, tiers, order, me, queries, gathered, gathered, gathered, gathered, w_out)


def local(
    residual_flow,
    tiers_each_segment,
    resident_tile_order,
    normalizer_weight_entries,
    lookup_map_weights,
    content_map_weights,
    softmax_warmth,
    attention_result_weight,
):
    tok_rows = residual_flow.shape[1]
    n_ctx = lax.axis_size("ctx")
    n_chips = n_ctx // 2
    me = lax.axis_index("ctx")
    core = me % 2
    half_rows = tok_rows // 2
    residual = residual_flow[0]
    residual_next = passed_along(residual_flow, "section", 1)

    own_block, queries = prologue(
        residual,
        normalizer_weight_entries[0],
        lookup_map_weights[0, 0],
        content_map_weights[0, 0],
    )
    own_block = lax.optimization_barrier(own_block)

    gathered = lax.all_gather(own_block, "ctx", axis=0, tiled=True)
    gathered, residual_next, queries = lax.optimization_barrier((gathered, residual_next, queries))

    update = attend_and_update(
        softmax_warmth[0, 0],
        tiers_each_segment,
        resident_tile_order,
        me.reshape(1).astype(jnp.int32),
        queries,
        gathered,
        attention_result_weight[0],
    )
    update = update.astype(jnp.float16)
    return residual_next + passed_along(update[None], "section", 1).astype(jnp.float32)


def solution(mesh):
    in_specs = (
        P("section", "ctx", None),
        P("section"),
        P(),
        P("section", None, None),
        P("section", None, None, None),
        P("section", None, None, None),
        P("section", None, None),
        P("section", None, None),
    )
    out_specs = P("section", "ctx", None)
    return jax.shard_map(local, mesh=mesh, in_specs=in_specs, out_specs=out_specs, check_vma=False)
```

```python
import functools

import jax
import jax.numpy as jnp
from jax import lax
from jax.experimental import pallas as pl
from jax.experimental.pallas import tpu as pltpu
from jax.sharding import PartitionSpec as P

H = 16
KEY_VALUE_HEADS = 4
ATTN_UNIT_WIDTH = 128


def passed_along(block, axis, distance):
    devices = range(lax.axis_size(axis))
    route = [((i - distance) % len(devices), i) for i in devices]
    return lax.ppermute(block, axis, route)


def head_norm(values):
    return values * lax.rsqrt(jnp.mean(values * values, axis=-1, keepdims=True) + 1e-05)


def attention_kernel(
    warmth_ref, tiers_ref, order_ref, me_ref, q_ref,
    ka_ref, va_ref, kb_ref, vb_ref, w_ref, out_ref,
):
    c = pl.program_id(0)
    group = q_ref.shape[1] // ATTN_UNIT_WIDTH
    rows = q_ref.shape[0]
    half = rows // 2
    kv_rows = ka_ref.shape[0]
    me = me_ref[0]
    r = lax.broadcasted_iota(jnp.int32, (rows, 1), 0)
    qpos = jnp.where(
        r < half, order_ref[2 * me] * half + r, order_ref[2 * me + 1] * half + r - half
    )
    j = lax.broadcasted_iota(jnp.int32, (1, kv_rows), 1)
    tile = j // half
    offset = j % half

    def key_positions(first_block):
        pos = offset
        for t in range(kv_rows // half):
            pos = pos + jnp.where(tile == t, order_ref[first_block + t] * half, 0)
        return pos

    allowed_a = key_positions(0) <= qpos
    allowed_b = key_positions(kv_rows // half) <= qpos
    ka = ka_ref[...]
    kb = kb_ref[...]
    va = va_ref[...]
    vb = vb_ref[...]
    gate = tiers_ref[0] > 0
    dims = (((1,), (1,)), ((), ()))
    for g in range(group):
        cols = slice(g * ATTN_UNIT_WIDTH, (g + 1) * ATTN_UNIT_WIDTH)
        qh = q_ref[:, cols]
        mult = warmth_ref[c * group + g] * (1.0 / ATTN_UNIT_WIDTH)
        s_a = jnp.where(allowed_a, lax.dot_general(qh, ka, dims, preferred_element_type=jnp.float32), -1e30)
        s_b = jnp.where(allowed_b, lax.dot_general(qh, kb, dims, preferred_element_type=jnp.float32), -1e30)
        row_max = jnp.maximum(
            jnp.max(s_a, axis=1, keepdims=True), jnp.max(s_b, axis=1, keepdims=True)
        ) * mult
        p_a = jnp.exp(s_a * mult - row_max)
        p_b = jnp.exp(s_b * mult - row_max)
        total = jnp.sum(p_a, axis=1, keepdims=True) + jnp.sum(p_b, axis=1, keepdims=True)
        mixed = jnp.dot(
            p_a.astype(jnp.bfloat16), va, preferred_element_type=jnp.float32
        ) + jnp.dot(p_b.astype(jnp.bfloat16), vb, preferred_element_type=jnp.float32)
        mixed = mixed * (1.0 / total)
        out_ref[:, cols] = jnp.where(gate, w_ref[:, cols] * mixed, 0.0).astype(out_ref.dtype)


def normed_rows(x_ref, gain_ref):
    x = x_ref[...]
    return (
        x * lax.rsqrt(jnp.mean(x * x, axis=1, keepdims=True) + 1e-05) * gain_ref[...]
    ).astype(jnp.bfloat16)


def key_value_kernel(x_ref, gain_ref, wk_ref, wv_ref, kv_ref):
    normed = normed_rows(x_ref, gain_ref)
    keys = jnp.dot(normed, wk_ref[...], preferred_element_type=jnp.float32)
    kv_cols = keys.shape[1]
    for c in range(kv_cols // ATTN_UNIT_WIDTH):
        cols = slice(c * ATTN_UNIT_WIDTH, (c + 1) * ATTN_UNIT_WIDTH)
        kv_ref[:, cols] = head_norm(keys[:, cols]).astype(jnp.bfloat16)
    kv_ref[:, kv_cols:] = jnp.dot(
        normed, wv_ref[...], preferred_element_type=jnp.float32
    ).astype(jnp.bfloat16)


def query_kernel(x_ref, gain_ref, q_ref):
    wide = normed_rows(x_ref, gain_ref).astype(jnp.float32)
    for h in range(wide.shape[1] // ATTN_UNIT_WIDTH):
        cols = slice(h * ATTN_UNIT_WIDTH, (h + 1) * ATTN_UNIT_WIDTH)
        q_ref[:, cols] = head_norm(wide[:, cols]).astype(jnp.bfloat16)


def prologue(x, gain, wk, wv):
    rows, width = x.shape
    kv_cols = wk.shape[1]
    own_block = pl.pallas_call(
        key_value_kernel,
        out_shape=jax.ShapeDtypeStruct((rows, 2 * kv_cols), jnp.bfloat16),
        cost_estimate=pl.CostEstimate(
            flops=4 * rows * width * kv_cols,
            transcendentals=rows * 8,
            bytes_accessed=2 * width * kv_cols * 2 + rows * width * 4 + rows * kv_cols * 4,
        ),
    )(x, gain, wk, wv)
    queries = pl.pallas_call(
        query_kernel,
        out_shape=jax.ShapeDtypeStruct((rows, width), jnp.bfloat16),
        cost_estimate=pl.CostEstimate(
            flops=8 * rows * width, transcendentals=rows * 20, bytes_accessed=rows * width * 6
        ),
    )(x, gain)
    return own_block, queries


def attend_and_update(warmth, tiers, order, me, queries, gathered, w_out):
    rows, width = queries.shape
    kv_rows = gathered.shape[0] // 2
    kv_heads = KEY_VALUE_HEADS
    head_cols = width // kv_heads
    smem = pl.BlockSpec(memory_space=pltpu.SMEM)
    whole = lambda shape: pl.BlockSpec(shape, lambda c: (0, 0))
    cols = lambda shape: pl.BlockSpec(shape, lambda c: (0, c))
    values_at = lambda shape: pl.BlockSpec(shape, lambda c: (0, c + kv_heads))
    late_keys = lambda shape: pl.BlockSpec(shape, lambda c: (1, c))
    late_values = lambda shape: pl.BlockSpec(shape, lambda c: (1, c + kv_heads))
    kv_block = (kv_rows, ATTN_UNIT_WIDTH)
    flops = 4 * rows * 2 * kv_rows * ATTN_UNIT_WIDTH * H
    return pl.pallas_call(
        attention_kernel,
        grid=(kv_heads,),
        in_specs=[
            smem,
            smem,
            smem,
            smem,
            cols((rows, head_cols)),
            cols(kv_block),
            values_at(kv_block),
            late_keys(kv_block),
            late_values(kv_block),
            cols((1, head_cols)),
        ],
        out_specs=cols((rows, head_cols)),
        out_shape=jax.ShapeDtypeStruct((rows, width), jnp.float32),
        cost_estimate=pl.CostEstimate(
            flops=flops,
            transcendentals=rows * 2 * kv_rows * H,
            bytes_accessed=4 * kv_rows * 1024 + rows * width * 10,
        ),
    )(warmth, tiers, order, me, queries, gathered, gathered, gathered, gathered, w_out)


def local(
    residual_flow,
    tiers_each_segment,
    resident_tile_order,
    normalizer_weight_entries,
    lookup_map_weights,
    content_map_weights,
    softmax_warmth,
    attention_result_weight,
):
    tok_rows = residual_flow.shape[1]
    n_ctx = lax.axis_size("ctx")
    n_chips = n_ctx // 2
    me = lax.axis_index("ctx")
    core = me % 2
    half_rows = tok_rows // 2
    residual = residual_flow[0]
    residual_next = passed_along(residual_flow, "section", 1)

    own_block, queries = prologue(
        residual,
        normalizer_weight_entries[0],
        lookup_map_weights[0, 0],
        content_map_weights[0, 0],
    )
    own_block = lax.optimization_barrier(own_block)

    gathered = lax.all_gather(own_block, "ctx", axis=0, tiled=True)
    gathered, residual_next, queries = lax.optimization_barrier((gathered, residual_next, queries))

    update = attend_and_update(
        softmax_warmth[0, 0],
        tiers_each_segment,
        resident_tile_order,
        me.reshape(1).astype(jnp.int32),
        queries,
        gathered,
        attention_result_weight[0],
    )
    update = update.astype(jnp.float16)
    return residual_next + passed_along(update[None], "section", 1).astype(jnp.float32)


def solution(mesh):
    in_specs = (
        P("section", "ctx", None),
        P("section"),
        P(),
        P("section", None, None),
        P("section", None, None, None),
        P("section", None, None, None),
        P("section", None, None),
        P("section", None, None),
    )
    out_specs = P("section", "ctx", None)
    return jax.shard_map(local, mesh=mesh, in_specs=in_specs, out_specs=out_specs, check_vma=False)
```
